128 devices in a mesh: seq: 32 (over z, y, core), head: 4 (over x).
Axes of the slice: x: 4, y: 4, z: 4, core: 2. Of those that a mesh axis runs over, the one named last changes fastest.
Arguments:
- queries: bfloat16 [32768, 4096], P(('seq', 'head')), may hold values from -6 to 6
- key_rows: bfloat16 [32768, 4096], P(('seq', 'head')), may hold values from -6 to 6
- value_rows: bfloat16 [32768, 4096], P(('seq', 'head')), may hold values from -6 to 6
- decay_rates: float32 [32], replicated, as said below
- norm_gain: float32 [4096], replicated, may hold values from 0.5 to 1.5
Outputs:
- attended: bfloat16 [32768, 4096], P(('seq', 'head'))
The draws below stay inside these ranges and needn't reach their ends.
Inputs may be any that keep to these rules, and one draw needn't show every extreme that they name: `decay_rates`: one positive rate per head.
All inputs are finite; a program needn't handle non-finite values.
Results may differ from the reference program's by a relative error of at most 0.003.
Values may be sent and summed in bfloat16 or wider, within the bound.
No kernel may reach another device: no remote copies, remote signals or barrier semaphores. Data moves between devices by JAX's collectives and lax.ppermute only.
A program may use at most 512 MiB of HBM per device.

```python
import math
import jax
import jax.numpy as jnp
from jax import lax

HEADS = 32
HEAD_DIM = 128
BLOCK = 256
TOKENS = 32768


def draw_decay_rates(key, part):
    pick_key, slow_key, fast_key = jax.random.split(key, 3)
    keep_share = 0.5
    slow = jnp.exp(jax.random.uniform(slow_key, (HEADS,), jnp.float32, math.log(0.1 / TOKENS), math.log(2.0 / TOKENS)))
    fast = jnp.exp(jax.random.uniform(fast_key, (HEADS,), jnp.float32, math.log(2.0 / TOKENS), math.log(1.0 / 30.0)))
    chosen = jax.random.bernoulli(pick_key, keep_share, (HEADS,))
    return jnp.where(chosen, slow, fast).astype(jnp.float32)


def steps_of(own_key, shape, cuts, low, high):
    gain, own = 1.0, jax.random.fold_in(own_key, 6)
    for dim, shards_of in cuts:
        heights = jnp.exp(jax.random.uniform(jax.random.fold_in(own, dim), (shards_of,), jnp.float32, low / len(cuts), high / len(cuts)))
        gain = gain * jnp.repeat(heights, shape[dim] // shards_of).reshape([-1 if axis == dim else 1 for axis in range(len(shape))])
    return gain


def bell_draw(rng, dims, spread, bound, cuts=(), kind=jnp.bfloat16):
    values = spread * jax.random.normal(rng, dims, jnp.float32)
    if cuts:
        values = values * steps_of(rng, dims, cuts, -0.22, 0.18)
    return jnp.clip(values, -bound, bound).astype(kind)


def setup_inputs(seed: int = 0) -> dict:
    arg_keys = jax.random.split(jax.random.key(seed), 6)
    return {
        "queries": bell_draw(arg_keys[0], (TOKENS, HEADS * HEAD_DIM), 1.0, 6.0, ((0, 128),)),
        "key_rows": bell_draw(arg_keys[1], (TOKENS, HEADS * HEAD_DIM), 1.0, 6.0, ((0, 128),)),
        "value_rows": bell_draw(arg_keys[2], (TOKENS, HEADS * HEAD_DIM), 1.0, 6.0, ((0, 128),)),
        "decay_rates": draw_decay_rates(jax.random.fold_in(arg_keys[5], 71), 0),
        "norm_gain": jnp.clip(1.0 + 0.1 * jax.random.normal(arg_keys[4], (HEADS * HEAD_DIM,), jnp.float32), 0.5, 1.5),
    }


def block_chain(queries, key_rows, value_rows, rates, block):
    tokens, heads, width = queries.shape
    count = tokens // block
    q_blocks = queries.reshape(count, block, heads, width)
    k_blocks = key_rows.reshape(count, block, heads, width)
    v_blocks = value_rows.reshape(count, block, heads, width)
    positions = jnp.arange(block, dtype=jnp.float32)
    offsets = positions[:, None] - positions[None, :]
    within = jnp.where(offsets[None] >= 0.0, jnp.exp(-rates[:, None, None] * jnp.maximum(offsets, 0.0)[None]), 0.0)
    q_decay = jnp.exp(-rates[None, :] * (positions[:, None] + 1.0))[:, :, None]
    k_decay = jnp.exp(-rates[None, :] * (block - 1.0 - positions[:, None]))[:, :, None]
    carry_decay = jnp.exp(-rates * block)[:, None, None]

    def advance(state, items):
        q_part, k_part, v_part = items
        q_wide = q_part.astype(jnp.float32)
        v_wide = v_part.astype(jnp.float32)
        scores = jnp.einsum('ihe,jhe->hij', q_wide, k_part.astype(jnp.float32))
        weights = (scores * within).astype(jnp.bfloat16)
        intra = jnp.einsum('hij,jhe->ihe', weights.astype(jnp.float32), v_wide)
        inter = jnp.einsum('ihe,hef->ihf', q_wide * q_decay, state, precision=lax.Precision.HIGHEST)
        added = jnp.einsum('jhe,jhf->hef', k_part.astype(jnp.float32) * k_decay, v_wide, precision=lax.Precision.HIGHEST)
        return (carry_decay * state + added, intra + inter)
    start = jnp.zeros((heads, width, width), jnp.float32)
    state, outputs = lax.scan(advance, start, (q_blocks, k_blocks, v_blocks))
    return (outputs.reshape(tokens, heads, width), state)

def reference(queries, key_rows, value_rows, decay_rates, norm_gain):
    shaped = (TOKENS, HEADS, HEAD_DIM)
    total, final_state = block_chain(queries.reshape(shaped), key_rows.reshape(shaped), value_rows.reshape(shaped), decay_rates, BLOCK)
    mean_square = lax.optimization_barrier(jnp.mean(total * total, axis=-1, keepdims=True))
    normed = total * lax.rsqrt(mean_square + 1e-06) * norm_gain.reshape(HEADS, HEAD_DIM)
    return normed.astype(jnp.bfloat16).reshape(TOKENS, HEADS * HEAD_DIM)
```

```python
import jax
import jax.numpy as jnp
from jax import lax
from jax.sharding import PartitionSpec as P

HEADS = 32
HEAD_DIM = 128
BLOCK = 256
AXES = ("seq", "head")


def split_hi_lo(x):
    hi = x.astype(jnp.bfloat16)
    lo = (x - hi.astype(jnp.float32)).astype(jnp.bfloat16)
    return hi, lo


def dot_f32(a_bf16, b_f32, spec):
    hi, lo = split_hi_lo(b_f32)
    return jnp.einsum(spec, a_bf16, hi, preferred_element_type=jnp.float32) + jnp.einsum(
        spec, a_bf16, lo, preferred_element_type=jnp.float32
    )


def body(n, queries, key_rows, value_rows, decay_rates, norm_gain):
    span = queries.shape[0]
    shaped = (span, HEADS, HEAD_DIM)
    q = queries.reshape(shaped)
    k = key_rows.reshape(shaped)
    v = value_rows.reshape(shaped)
    me = lax.axis_index(AXES)

    positions = jnp.arange(span, dtype=jnp.float32)
    offsets = positions[:, None] - positions[None, :]
    within = jnp.where(
        offsets[None] >= 0.0,
        jnp.exp(-decay_rates[:, None, None] * jnp.maximum(offsets, 0.0)[None]),
        0.0,
    )
    q_decay = jnp.exp(-decay_rates[None, :] * (positions[:, None] + 1.0))[:, :, None]
    k_decay = jnp.exp(-decay_rates[None, :] * (span - 1.0 - positions[:, None]))[:, :, None]

    local_state = dot_f32(v, k.astype(jnp.float32) * k_decay, "jhf,jhe->hef")

    rows = HEADS * HEAD_DIM // n
    chunks = local_state.reshape(n, rows, HEAD_DIM)
    gathered = lax.all_to_all(chunks, AXES, 0, 0, tiled=True)
    head_of_chunk = me // (n // HEADS)
    rate = lax.dynamic_slice_in_dim(decay_rates, head_of_chunk, 1)[0]
    blocks = jnp.arange(n, dtype=jnp.float32)
    gaps = blocks[:, None] - 1.0 - blocks[None, :]
    chain = jnp.where(
        gaps >= 0.0, jnp.exp(-rate * float(span) * jnp.maximum(gaps, 0.0)), 0.0
    )
    before = jnp.einsum(
        "ab,bxy->axy", chain, gathered, precision=lax.Precision.HIGHEST
    )
    incoming = lax.all_to_all(before, AXES, 0, 0, tiled=True).reshape(
        HEADS, HEAD_DIM, HEAD_DIM
    )

    scores = jnp.einsum("ihe,jhe->hij", q, k, preferred_element_type=jnp.float32)
    weights = (scores * within).astype(jnp.bfloat16)
    intra = jnp.einsum("hij,jhe->ihe", weights, v, preferred_element_type=jnp.float32)
    inter = dot_f32(q, incoming, "ihe,hef->ihf") * q_decay
    total = intra + inter

    mean_square = jnp.mean(total * total, axis=-1, keepdims=True)
    gains = norm_gain.reshape(HEADS, HEAD_DIM)
    normed = (total * lax.rsqrt(mean_square + 1e-06) * gains).astype(jnp.bfloat16)
    return normed.reshape(span, HEADS * HEAD_DIM)


def solution(mesh):
    n = mesh.shape["seq"] * mesh.shape["head"]

    def run(queries, key_rows, value_rows, decay_rates, norm_gain):
        return body(n, queries, key_rows, value_rows, decay_rates, norm_gain)

    return jax.shard_map(
        run,
        mesh=mesh,
        in_specs=(
            P(AXES, None),
            P(AXES, None),
            P(AXES, None),
            P(),
            P(),
        ),
        out_specs=P(AXES, None),
        check_vma=False,
    )
```

```python
import jax
import jax.numpy as jnp
from jax import lax
from jax.sharding import PartitionSpec as P

HEADS = 32
HEAD_DIM = 128
BLOCK = 256
AXES = ("seq", "head")


def split_hi_lo(x):
    hi = lax.reduce_precision(x, exponent_bits=8, mantissa_bits=7)
    return hi.astype(jnp.bfloat16), (x - hi).astype(jnp.bfloat16)


def dot_f32(a_bf16, b_f32, spec):
    hi, lo = split_hi_lo(b_f32)
    return jnp.einsum(spec, a_bf16, hi, preferred_element_type=jnp.float32) + jnp.einsum(
        spec, a_bf16, lo, preferred_element_type=jnp.float32
    )


def body(n, queries, key_rows, value_rows, decay_rates, norm_gain):
    span = queries.shape[0]
    shaped = (span, HEADS, HEAD_DIM)
    q = queries.reshape(shaped)
    k = key_rows.reshape(shaped)
    v = value_rows.reshape(shaped)
    me = lax.axis_index(AXES)

    positions = jnp.arange(span, dtype=jnp.float32)
    offsets = positions[:, None] - positions[None, :]
    within = jnp.where(
        offsets[None] >= 0.0,
        jnp.exp(-decay_rates[:, None, None] * jnp.maximum(offsets, 0.0)[None]),
        0.0,
    )
    q_decay = jnp.exp(-decay_rates[None, :] * (positions[:, None] + 1.0))[:, :, None]
    k_decay = jnp.exp(-decay_rates[None, :] * (span - 1.0 - positions[:, None]))[:, :, None]

    local_state = dot_f32(v, k.astype(jnp.float32) * k_decay, "jhf,jhe->hef")

    rows = HEADS * HEAD_DIM // n
    chunks = local_state.reshape(n, rows, HEAD_DIM)
    gathered = lax.all_to_all(chunks, AXES, 0, 0, tiled=True)
    head_of_chunk = me // (n // HEADS)
    rate = lax.dynamic_slice_in_dim(decay_rates, head_of_chunk, 1)[0]
    blocks = jnp.arange(n, dtype=jnp.float32)
    gaps = blocks[:, None] - 1.0 - blocks[None, :]
    chain = jnp.where(
        gaps >= 0.0, jnp.exp(-rate * float(span) * jnp.maximum(gaps, 0.0)), 0.0
    )
    before = jnp.einsum(
        "ab,bxy->axy", chain, gathered, precision=lax.Precision.HIGHEST
    )
    incoming = lax.all_to_all(before, AXES, 0, 0, tiled=True).reshape(
        HEADS, HEAD_DIM, HEAD_DIM
    )

    scores = jnp.einsum("ihe,jhe->hij", q, k, preferred_element_type=jnp.float32)
    weights = (scores * within).astype(jnp.bfloat16)
    intra = jnp.einsum("hij,jhe->ihe", weights, v, preferred_element_type=jnp.float32)
    inter = dot_f32(q, incoming, "ihe,hef->ihf") * q_decay
    total = intra + inter

    mean_square = jnp.mean(total * total, axis=-1, keepdims=True)
    gains = norm_gain.reshape(HEADS, HEAD_DIM)
    normed = (total * lax.rsqrt(mean_square + 1e-06) * gains).astype(jnp.bfloat16)
    return normed.reshape(span, HEADS * HEAD_DIM)


def solution(mesh):
    n = mesh.shape["seq"] * mesh.shape["head"]

    def run(queries, key_rows, value_rows, decay_rates, norm_gain):
        return body(n, queries, key_rows, value_rows, decay_rates, norm_gain)

    return jax.shard_map(
        run,
        mesh=mesh,
        in_specs=(
            P(AXES, None),
            P(AXES, None),
            P(AXES, None),
            P(),
            P(),
        ),
        out_specs=P(AXES, None),
        check_vma=False,
    )
```

```python
import jax
import jax.numpy as jnp
from jax import lax
from jax.experimental import pallas as pl
from jax.experimental.pallas import tpu as pltpu
from jax.sharding import PartitionSpec as P

HEADS = 32
HEAD_DIM = 128
BLOCK = 256
AXES = ("seq", "head")
GROUP = 8


def split_hi_lo(x):
    hi = lax.reduce_precision(x, exponent_bits=8, mantissa_bits=7)
    return hi.astype(jnp.bfloat16), (x - hi).astype(jnp.bfloat16)


def kernel_split(x):
    hi = x.astype(jnp.bfloat16)
    return hi, (x - hi.astype(jnp.float32)).astype(jnp.bfloat16)


def state_kernel(rates_ref, k_ref, v_ref, out_ref):
    g = pl.program_id(0)
    span = k_ref.shape[0]
    tail = (span - 1.0) - lax.broadcasted_iota(jnp.int32, (span, 1), 0).astype(jnp.float32)
    for hh in range(GROUP):
        rate = rates_ref[g * GROUP + hh]
        cols = slice(hh * HEAD_DIM, (hh + 1) * HEAD_DIM)
        kd = k_ref[:, cols].astype(jnp.float32) * jnp.exp(-rate * tail)
        hi, lo = kernel_split(kd)
        v = v_ref[:, cols]
        dims = (((0,), (0,)), ((), ()))
        out_ref[hh] = lax.dot_general(
            hi, v, dims, preferred_element_type=jnp.float32
        ) + lax.dot_general(lo, v, dims, preferred_element_type=jnp.float32)


def block_state(decay_rates, k, v):
    span = k.shape[0]
    groups = HEADS // GROUP
    width = GROUP * HEAD_DIM
    return pl.pallas_call(
        state_kernel,
        grid=(groups,),
        in_specs=[
            pl.BlockSpec(memory_space=pltpu.SMEM),
            pl.BlockSpec((span, width), lambda g: (0, g)),
            pl.BlockSpec((span, width), lambda g: (0, g)),
        ],
        out_specs=pl.BlockSpec((GROUP, HEAD_DIM, HEAD_DIM), lambda g: (g, 0, 0)),
        out_shape=jax.ShapeDtypeStruct((HEADS, HEAD_DIM, HEAD_DIM), jnp.float32),
        cost_estimate=pl.CostEstimate(
            flops=4 * span * HEADS * HEAD_DIM * HEAD_DIM,
            transcendentals=span * HEADS * HEAD_DIM,
            bytes_accessed=2 * 2 * span * HEADS * HEAD_DIM + 4 * HEADS * HEAD_DIM * HEAD_DIM,
        ),
    )(decay_rates, k, v)


def output_kernel(rates_ref, q_ref, k_ref, v_ref, s_ref, gain_ref, out_ref):
    g = pl.program_id(0)
    span = q_ref.shape[0]
    rows = lax.broadcasted_iota(jnp.int32, (span, span), 0).astype(jnp.float32)
    cols_i = lax.broadcasted_iota(jnp.int32, (span, span), 1).astype(jnp.float32)
    offsets = rows - cols_i
    causal = offsets >= 0.0
    gap = jnp.maximum(offsets, 0.0)
    lead = lax.broadcasted_iota(jnp.int32, (span, 1), 0).astype(jnp.float32) + 1.0
    for hh in range(GROUP):
        rate = rates_ref[g * GROUP + hh]
        cols = slice(hh * HEAD_DIM, (hh + 1) * HEAD_DIM)
        q = q_ref[:, cols]
        k = k_ref[:, cols]
        v = v_ref[:, cols]
        scores = lax.dot_general(
            q, k, (((1,), (1,)), ((), ())), preferred_element_type=jnp.float32
        )
        within = jnp.where(causal, jnp.exp(-rate * gap), 0.0)
        weights = (scores * within).astype(jnp.bfloat16)
        intra = jnp.dot(weights, v, preferred_element_type=jnp.float32)
        hi, lo = kernel_split(s_ref[hh])
        inter = jnp.dot(q, hi, preferred_element_type=jnp.float32) + jnp.dot(
            q, lo, preferred_element_type=jnp.float32
        )
        total = intra + inter * jnp.exp(-rate * lead)
        mean_square = jnp.mean(total * total, axis=-1, keepdims=True)
        normed = total * lax.rsqrt(mean_square + 1e-06) * gain_ref[hh : hh + 1, :]
        out_ref[:, cols] = normed.astype(out_ref.dtype)


def block_output(decay_rates, q, k, v, incoming, gains):
    span = q.shape[0]
    groups = HEADS // GROUP
    width = GROUP * HEAD_DIM
    return pl.pallas_call(
        output_kernel,
        grid=(groups,),
        in_specs=[
            pl.BlockSpec(memory_space=pltpu.SMEM),
            pl.BlockSpec((span, width), lambda g: (0, g)),
            pl.BlockSpec((span, width), lambda g: (0, g)),
            pl.BlockSpec((span, width), lambda g: (0, g)),
            pl.BlockSpec((GROUP, HEAD_DIM, HEAD_DIM), lambda g: (g, 0, 0)),
            pl.BlockSpec((GROUP, HEAD_DIM), lambda g: (g, 0)),
        ],
        out_specs=pl.BlockSpec((span, width), lambda g: (0, g)),
        out_shape=jax.ShapeDtypeStruct((span, HEADS * HEAD_DIM), jnp.bfloat16),
        cost_estimate=pl.CostEstimate(
            flops=HEADS * (4 * span * span * HEAD_DIM + 4 * span * HEAD_DIM * HEAD_DIM),
            transcendentals=HEADS * span * span,
            bytes_accessed=4 * 2 * span * HEADS * HEAD_DIM + 4 * HEADS * HEAD_DIM * HEAD_DIM,
        ),
    )(decay_rates, q, k, v, incoming, gains)


def body(n, queries, key_rows, value_rows, decay_rates, norm_gain):
    span = queries.shape[0]
    me = lax.axis_index(AXES)

    local_state = block_state(decay_rates, key_rows, value_rows)

    rows = HEADS * HEAD_DIM // n
    chunks = local_state.reshape(n, rows, HEAD_DIM)
    gathered = lax.all_to_all(chunks, AXES, 0, 0, tiled=True)
    head_of_chunk = me // (n // HEADS)
    rate = lax.dynamic_slice_in_dim(decay_rates, head_of_chunk, 1)[0]
    blocks = jnp.arange(n, dtype=jnp.float32)
    gaps = blocks[:, None] - 1.0 - blocks[None, :]
    chain = jnp.where(
        gaps >= 0.0, jnp.exp(-rate * float(span) * jnp.maximum(gaps, 0.0)), 0.0
    )
    c_hi, c_lo = split_hi_lo(chain)
    g_hi, g_lo = split_hi_lo(gathered)
    spec = "ab,bxy->axy"
    before = (
        jnp.einsum(spec, c_hi, g_hi, preferred_element_type=jnp.float32)
        + jnp.einsum(spec, c_lo, g_hi, preferred_element_type=jnp.float32)
        + jnp.einsum(spec, c_hi, g_lo, preferred_element_type=jnp.float32)
    )
    incoming = lax.all_to_all(before, AXES, 0, 0, tiled=True).reshape(
        HEADS, HEAD_DIM, HEAD_DIM
    )

    gains = norm_gain.reshape(HEADS, HEAD_DIM)
    return block_output(decay_rates, queries, key_rows, value_rows, incoming, gains)


def solution(mesh):
    n = mesh.shape["seq"] * mesh.shape["head"]

    def run(queries, key_rows, value_rows, decay_rates, norm_gain):
        return body(n, queries, key_rows, value_rows, decay_rates, norm_gain)

    return jax.shard_map(
        run,
        mesh=mesh,
        in_specs=(
            P(AXES, None),
            P(AXES, None),
            P(AXES, None),
            P(),
            P(),
        ),
        out_specs=P(AXES, None),
        check_vma=False,
    )
```

```python
import jax
import jax.numpy as jnp
from jax import lax
from jax.experimental import pallas as pl
from jax.experimental.pallas import tpu as pltpu
from jax.sharding import PartitionSpec as P

HEADS = 32
HEAD_DIM = 128
BLOCK = 256
AXES = ("seq", "head")
GROUP = 8
CHAIN_BLOCKS = 128


def split_hi_lo(x):
    hi = lax.reduce_precision(x, exponent_bits=8, mantissa_bits=7)
    return hi.astype(jnp.bfloat16), (x - hi).astype(jnp.bfloat16)


def kernel_split(x):
    hi = x.astype(jnp.bfloat16)
    return hi, (x - hi.astype(jnp.float32)).astype(jnp.bfloat16)


def state_kernel(rates_ref, k_ref, v_ref, out_ref):
    g = pl.program_id(0)
    span = k_ref.shape[0]
    tail = (span - 1.0) - lax.broadcasted_iota(jnp.int32, (span, 1), 0).astype(jnp.float32)
    for hh in range(GROUP):
        rate = rates_ref[g * GROUP + hh]
        cols = slice(hh * HEAD_DIM, (hh + 1) * HEAD_DIM)
        kd = k_ref[:, cols].astype(jnp.float32) * jnp.exp(-rate * tail)
        hi, lo = kernel_split(kd)
        v = v_ref[:, cols]
        dims = (((0,), (0,)), ((), ()))
        out_ref[hh] = lax.dot_general(
            hi, v, dims, preferred_element_type=jnp.float32
        ) + lax.dot_general(lo, v, dims, preferred_element_type=jnp.float32)


def block_state(decay_rates, k, v):
    span = k.shape[0]
    groups = HEADS // GROUP
    width = GROUP * HEAD_DIM
    return pl.pallas_call(
        state_kernel,
        grid=(groups,),
        in_specs=[
            pl.BlockSpec(memory_space=pltpu.SMEM),
            pl.BlockSpec((span, width), lambda g: (0, g)),
            pl.BlockSpec((span, width), lambda g: (0, g)),
        ],
        out_specs=pl.BlockSpec((GROUP, HEAD_DIM, HEAD_DIM), lambda g: (g, 0, 0)),
        out_shape=jax.ShapeDtypeStruct((HEADS, HEAD_DIM, HEAD_DIM), jnp.float32),
        cost_estimate=pl.CostEstimate(
            flops=4 * span * HEADS * HEAD_DIM * HEAD_DIM,
            transcendentals=span * HEADS * HEAD_DIM,
            bytes_accessed=2 * 2 * span * HEADS * HEAD_DIM + 4 * HEADS * HEAD_DIM * HEAD_DIM,
        ),
    )(decay_rates, k, v)


def intra_kernel(rates_ref, q_ref, k_ref, v_ref, out_ref):
    g = pl.program_id(0)
    span = q_ref.shape[0]
    rows = lax.broadcasted_iota(jnp.int32, (span, span), 0).astype(jnp.float32)
    cols_i = lax.broadcasted_iota(jnp.int32, (span, span), 1).astype(jnp.float32)
    offsets = rows - cols_i
    causal = offsets >= 0.0
    gap = jnp.maximum(offsets, 0.0)
    for hh in range(GROUP):
        rate = rates_ref[g * GROUP + hh]
        cols = slice(hh * HEAD_DIM, (hh + 1) * HEAD_DIM)
        q = q_ref[:, cols]
        k = k_ref[:, cols]
        scores = lax.dot_general(
            q, k, (((1,), (1,)), ((), ())), preferred_element_type=jnp.float32
        )
        within = jnp.where(causal, jnp.exp(-rate * gap), 0.0)
        weights = (scores * within).astype(jnp.bfloat16)
        out_ref[:, cols] = jnp.dot(weights, v_ref[:, cols], preferred_element_type=jnp.float32)


def block_intra(decay_rates, q, k, v):
    span = q.shape[0]
    groups = HEADS // GROUP
    width = GROUP * HEAD_DIM
    return pl.pallas_call(
        intra_kernel,
        grid=(groups,),
        in_specs=[
            pl.BlockSpec(memory_space=pltpu.SMEM),
            pl.BlockSpec((span, width), lambda g: (0, g)),
            pl.BlockSpec((span, width), lambda g: (0, g)),
            pl.BlockSpec((span, width), lambda g: (0, g)),
        ],
        out_specs=pl.BlockSpec((span, width), lambda g: (0, g)),
        out_shape=jax.ShapeDtypeStruct((span, HEADS * HEAD_DIM), jnp.float32),
        cost_estimate=pl.CostEstimate(
            flops=HEADS * 4 * span * span * HEAD_DIM,
            transcendentals=HEADS * span * span,
            bytes_accessed=3 * 2 * span * HEADS * HEAD_DIM + 4 * span * HEADS * HEAD_DIM,
        ),
    )(decay_rates, q, k, v)


def output_kernel(rates_ref, intra_ref, q_ref, s_ref, gain_ref, out_ref):
    g = pl.program_id(0)
    span = q_ref.shape[0]
    lead = lax.broadcasted_iota(jnp.int32, (span, 1), 0).astype(jnp.float32) + 1.0
    for hh in range(GROUP):
        rate = rates_ref[g * GROUP + hh]
        cols = slice(hh * HEAD_DIM, (hh + 1) * HEAD_DIM)
        q = q_ref[:, cols]
        hi, lo = kernel_split(s_ref[hh])
        inter = jnp.dot(q, hi, preferred_element_type=jnp.float32) + jnp.dot(
            q, lo, preferred_element_type=jnp.float32
        )
        total = intra_ref[:, cols] + inter * jnp.exp(-rate * lead)
        mean_square = jnp.mean(total * total, axis=-1, keepdims=True)
        normed = total * lax.rsqrt(mean_square + 1e-06) * gain_ref[hh : hh + 1, :]
        out_ref[:, cols] = normed.astype(out_ref.dtype)


def block_output(decay_rates, intra, q, incoming, gains):
    span = q.shape[0]
    groups = HEADS // GROUP
    width = GROUP * HEAD_DIM
    return pl.pallas_call(
        output_kernel,
        grid=(groups,),
        in_specs=[
            pl.BlockSpec(memory_space=pltpu.SMEM),
            pl.BlockSpec((span, width), lambda g: (0, g)),
            pl.BlockSpec((span, width), lambda g: (0, g)),
            pl.BlockSpec((GROUP, HEAD_DIM, HEAD_DIM), lambda g: (g, 0, 0)),
            pl.BlockSpec((GROUP, HEAD_DIM), lambda g: (g, 0)),
        ],
        out_specs=pl.BlockSpec((span, width), lambda g: (0, g)),
        out_shape=jax.ShapeDtypeStruct((span, HEADS * HEAD_DIM), jnp.bfloat16),
        cost_estimate=pl.CostEstimate(
            flops=HEADS * 4 * span * HEAD_DIM * HEAD_DIM,
            transcendentals=HEADS * span,
            bytes_accessed=8 * span * HEADS * HEAD_DIM + 4 * HEADS * HEAD_DIM * HEAD_DIM,
        ),
    )(decay_rates, intra, q, incoming, gains)


def chain_kernel(scale_ref, g_ref, out_ref):
    blocks = CHAIN_BLOCKS
    parts = g_ref.shape[0] // blocks
    scale = scale_ref[0]
    a = lax.broadcasted_iota(jnp.int32, (blocks, blocks), 0).astype(jnp.float32)
    b = lax.broadcasted_iota(jnp.int32, (blocks, blocks), 1).astype(jnp.float32)
    gaps = a - 1.0 - b
    chain = jnp.where(gaps >= 0.0, jnp.exp(-scale * jnp.maximum(gaps, 0.0)), 0.0)
    c_hi, c_lo = kernel_split(chain)
    for r in range(parts):
        x = g_ref[pl.ds(r, blocks, stride=parts), :]
        x_hi, x_lo = kernel_split(x)
        y = (
            jnp.dot(c_hi, x_hi, preferred_element_type=jnp.float32)
            + jnp.dot(c_lo, x_hi, preferred_element_type=jnp.float32)
            + jnp.dot(c_hi, x_lo, preferred_element_type=jnp.float32)
        )
        out_ref[pl.ds(r, blocks, stride=parts), :] = y


def block_chain(scale, gathered2d):
    blocks = CHAIN_BLOCKS
    rows, width = gathered2d.shape
    return pl.pallas_call(
        chain_kernel,
        in_specs=[
            pl.BlockSpec(memory_space=pltpu.SMEM),
            pl.BlockSpec((rows, width), lambda: (0, 0)),
        ],
        out_specs=pl.BlockSpec((rows, width), lambda: (0, 0)),
        out_shape=jax.ShapeDtypeStruct((rows, width), jnp.float32),
        cost_estimate=pl.CostEstimate(
            flops=6 * blocks * rows * width,
            transcendentals=blocks * blocks,
            bytes_accessed=8 * rows * width,
        ),
    )(scale, gathered2d)


def body(n, queries, key_rows, value_rows, decay_rates, norm_gain):
    span = queries.shape[0]
    me = lax.axis_index(AXES)

    local_state = block_state(decay_rates, key_rows, value_rows)

    rows = HEADS * HEAD_DIM // n
    chunks = local_state.reshape(n, rows, HEAD_DIM)
    gathered = lax.all_to_all(chunks, AXES, 0, 0, tiled=True)
    intra = block_intra(decay_rates, queries, key_rows, value_rows)
    head_of_chunk = me // (n // HEADS)
    rate = lax.dynamic_slice_in_dim(decay_rates, head_of_chunk, 1)
    before = block_chain(rate * float(span), gathered.reshape(n * rows, HEAD_DIM))
    incoming = lax.all_to_all(before.reshape(n, rows, HEAD_DIM), AXES, 0, 0, tiled=True)
    incoming = incoming.reshape(HEADS, HEAD_DIM, HEAD_DIM)

    gains = norm_gain.reshape(HEADS, HEAD_DIM)
    return block_output(decay_rates, intra, queries, incoming, gains)


def solution(mesh):
    n = mesh.shape["seq"] * mesh.shape["head"]

    def run(queries, key_rows, value_rows, decay_rates, norm_gain):
        return body(n, queries, key_rows, value_rows, decay_rates, norm_gain)

    return jax.shard_map(
        run,
        mesh=mesh,
        in_specs=(
            P(AXES, None),
            P(AXES, None),
            P(AXES, None),
            P(),
            P(),
        ),
        out_specs=P(AXES, None),
        check_vma=False,
    )
```

```python
import jax
import jax.numpy as jnp
from jax import lax
from jax.experimental import pallas as pl
from jax.experimental.pallas import tpu as pltpu
from jax.sharding import PartitionSpec as P

HEADS = 32
HEAD_DIM = 128
BLOCK = 256
AXES = ("seq", "head")
GROUP = 8


def split_hi_lo(x):
    hi = lax.reduce_precision(x, exponent_bits=8, mantissa_bits=7)
    return hi.astype(jnp.bfloat16), (x - hi).astype(jnp.bfloat16)


def kernel_split(x):
    hi = x.astype(jnp.bfloat16)
    return hi, (x - hi.astype(jnp.float32)).astype(jnp.bfloat16)


def state_kernel(rates_ref, k_ref, v_ref, out_ref):
    g = pl.program_id(0)
    span = k_ref.shape[0]
    tail = (span - 1.0) - lax.broadcasted_iota(jnp.int32, (span, 1), 0).astype(jnp.float32)
    for hh in range(GROUP):
        rate = rates_ref[g * GROUP + hh]
        cols = slice(hh * HEAD_DIM, (hh + 1) * HEAD_DIM)
        kd = k_ref[:, cols].astype(jnp.float32) * jnp.exp(-rate * tail)
        hi, lo = kernel_split(kd)
        v = v_ref[:, cols]
        dims = (((0,), (0,)), ((), ()))
        out_ref[hh] = lax.dot_general(
            hi, v, dims, preferred_element_type=jnp.float32
        ) + lax.dot_general(lo, v, dims, preferred_element_type=jnp.float32)


def block_state(decay_rates, k, v):
    span = k.shape[0]
    groups = HEADS // GROUP
    width = GROUP * HEAD_DIM
    return pl.pallas_call(
        state_kernel,
        grid=(groups,),
        in_specs=[
            pl.BlockSpec(memory_space=pltpu.SMEM),
            pl.BlockSpec((span, width), lambda g: (0, g)),
            pl.BlockSpec((span, width), lambda g: (0, g)),
        ],
        out_specs=pl.BlockSpec((GROUP, HEAD_DIM, HEAD_DIM), lambda g: (g, 0, 0)),
        out_shape=jax.ShapeDtypeStruct((HEADS, HEAD_DIM, HEAD_DIM), jnp.float32),
        cost_estimate=pl.CostEstimate(
            flops=4 * span * HEADS * HEAD_DIM * HEAD_DIM,
            transcendentals=span * HEADS * HEAD_DIM,
            bytes_accessed=2 * 2 * span * HEADS * HEAD_DIM + 4 * HEADS * HEAD_DIM * HEAD_DIM,
        ),
    )(decay_rates, k, v)


def intra_kernel(rates_ref, q_ref, k_ref, v_ref, out_ref):
    g = pl.program_id(0)
    span = q_ref.shape[0]
    rows = lax.broadcasted_iota(jnp.int32, (span, span), 0).astype(jnp.float32)
    cols_i = lax.broadcasted_iota(jnp.int32, (span, span), 1).astype(jnp.float32)
    offsets = rows - cols_i
    causal = offsets >= 0.0
    gap = jnp.maximum(offsets, 0.0)
    for hh in range(GROUP):
        rate = rates_ref[g * GROUP + hh]
        cols = slice(hh * HEAD_DIM, (hh + 1) * HEAD_DIM)
        q = q_ref[:, cols]
        k = k_ref[:, cols]
        scores = lax.dot_general(
            q, k, (((1,), (1,)), ((), ())), preferred_element_type=jnp.float32
        )
        within = jnp.where(causal, jnp.exp(-rate * gap), 0.0)
        weights = (scores * within).astype(jnp.bfloat16)
        out_ref[:, cols] = jnp.dot(weights, v_ref[:, cols], preferred_element_type=jnp.float32)


def block_intra(decay_rates, q, k, v):
    span = q.shape[0]
    groups = HEADS // GROUP
    width = GROUP * HEAD_DIM
    return pl.pallas_call(
        intra_kernel,
        grid=(groups,),
        in_specs=[
            pl.BlockSpec(memory_space=pltpu.SMEM),
            pl.BlockSpec((span, width), lambda g: (0, g)),
            pl.BlockSpec((span, width), lambda g: (0, g)),
            pl.BlockSpec((span, width), lambda g: (0, g)),
        ],
        out_specs=pl.BlockSpec((span, width), lambda g: (0, g)),
        out_shape=jax.ShapeDtypeStruct((span, HEADS * HEAD_DIM), jnp.float32),
        cost_estimate=pl.CostEstimate(
            flops=HEADS * 4 * span * span * HEAD_DIM,
            transcendentals=HEADS * span * span,
            bytes_accessed=3 * 2 * span * HEADS * HEAD_DIM + 4 * span * HEADS * HEAD_DIM,
        ),
    )(decay_rates, q, k, v)


def output_kernel(rates_ref, intra_ref, q_ref, s_ref, gain_ref, out_ref):
    g = pl.program_id(0)
    span = q_ref.shape[0]
    lead = lax.broadcasted_iota(jnp.int32, (span, 1), 0).astype(jnp.float32) + 1.0
    for hh in range(GROUP):
        rate = rates_ref[g * GROUP + hh]
        cols = slice(hh * HEAD_DIM, (hh + 1) * HEAD_DIM)
        q = q_ref[:, cols]
        hi, lo = kernel_split(s_ref[g * GROUP + hh])
        inter = jnp.dot(q, hi, preferred_element_type=jnp.float32) + jnp.dot(
            q, lo, preferred_element_type=jnp.float32
        )
        total = intra_ref[:, cols] + inter * jnp.exp(-rate * lead)
        mean_square = jnp.mean(total * total, axis=-1, keepdims=True)
        normed = total * lax.rsqrt(mean_square + 1e-06) * gain_ref[hh : hh + 1, :]
        out_ref[:, cols] = normed.astype(out_ref.dtype)


def block_output(decay_rates, intra, q, incoming, gains):
    span = q.shape[0]
    groups = HEADS // GROUP
    width = GROUP * HEAD_DIM
    return pl.pallas_call(
        output_kernel,
        grid=(groups,),
        in_specs=[
            pl.BlockSpec(memory_space=pltpu.SMEM),
            pl.BlockSpec((span, width), lambda g: (0, g)),
            pl.BlockSpec((span, width), lambda g: (0, g)),
            pl.BlockSpec(memory_space=pltpu.VMEM),
            pl.BlockSpec((GROUP, HEAD_DIM), lambda g: (g, 0)),
        ],
        out_specs=pl.BlockSpec((span, width), lambda g: (0, g)),
        out_shape=jax.ShapeDtypeStruct((span, HEADS * HEAD_DIM), jnp.bfloat16),
        cost_estimate=pl.CostEstimate(
            flops=HEADS * 4 * span * HEAD_DIM * HEAD_DIM,
            transcendentals=HEADS * span,
            bytes_accessed=8 * span * HEADS * HEAD_DIM + 4 * HEADS * HEAD_DIM * HEAD_DIM,
        ),
    )(decay_rates, intra, q, incoming, gains)


def chain_kernel(carry_ref, g_ref, out_ref):
    carry = carry_ref[0]
    state = jnp.zeros(out_ref.shape[1:], jnp.float32)
    out_ref[0] = state

    def step(b, state):
        state = carry * state + g_ref[b - 1]
        out_ref[b] = state
        return state

    lax.fori_loop(1, out_ref.shape[0], step, state, unroll=8)


def block_chain(carry, gathered):
    blocks, rows, width = gathered.shape
    return pl.pallas_call(
        chain_kernel,
        in_specs=[
            pl.BlockSpec(memory_space=pltpu.SMEM),
            pl.BlockSpec(memory_space=pltpu.VMEM),
        ],
        out_specs=pl.BlockSpec(memory_space=pltpu.VMEM),
        out_shape=jax.ShapeDtypeStruct((blocks, rows, width), jnp.float32),
        cost_estimate=pl.CostEstimate(
            flops=2 * blocks * rows * width,
            transcendentals=0,
            bytes_accessed=8 * blocks * rows * width,
        ),
    )(carry, gathered)


def body(n, queries, key_rows, value_rows, decay_rates, norm_gain):
    span = queries.shape[0]
    me = lax.axis_index(AXES)

    local_state = block_state(decay_rates, key_rows, value_rows)

    rows = HEADS * HEAD_DIM // n
    chunks = local_state.reshape(n, rows, HEAD_DIM)
    gathered = lax.all_to_all(chunks, AXES, 0, 0, tiled=True)
    intra = block_intra(decay_rates, queries, key_rows, value_rows)
    head_of_chunk = me // (n // HEADS)
    rate = lax.dynamic_slice_in_dim(decay_rates, head_of_chunk, 1)
    before = block_chain(jnp.exp(-rate * float(span)), gathered)
    incoming = lax.all_to_all(before, AXES, 0, 0, tiled=True)
    incoming = incoming.reshape(HEADS, HEAD_DIM, HEAD_DIM)

    gains = norm_gain.reshape(HEADS, HEAD_DIM)
    return block_output(decay_rates, intra, queries, incoming, gains)


def solution(mesh):
    n = mesh.shape["seq"] * mesh.shape["head"]

    def run(queries, key_rows, value_rows, decay_rates, norm_gain):
        return body(n, queries, key_rows, value_rows, decay_rates, norm_gain)

    return jax.shard_map(
        run,
        mesh=mesh,
        in_specs=(
            P(AXES, None),
            P(AXES, None),
            P(AXES, None),
            P(),
            P(),
        ),
        out_specs=P(AXES, None),
        check_vma=False,
    )
```

```python
import jax
import jax.numpy as jnp
from jax import lax
from jax.experimental import pallas as pl
from jax.experimental.pallas import tpu as pltpu
from jax.sharding import PartitionSpec as P

HEADS = 32
HEAD_DIM = 128
BLOCK = 256
AXES = ("seq", "head")
GROUP = 8
PIECE = 64


def split_hi_lo(x):
    hi = lax.reduce_precision(x, exponent_bits=8, mantissa_bits=7)
    return hi.astype(jnp.bfloat16), (x - hi).astype(jnp.bfloat16)


def kernel_split(x):
    hi = x.astype(jnp.bfloat16)
    return hi, (x - hi.astype(jnp.float32)).astype(jnp.bfloat16)


def state_kernel(rates_ref, k_ref, v_ref, out_ref):
    g = pl.program_id(0)
    span = k_ref.shape[0]
    dims = (((0,), (0,)), ((), ()))

    def head(hh, carry):
        rate = rates_ref[g * GROUP + hh]
        cols = pl.ds(pl.multiple_of(hh * HEAD_DIM, HEAD_DIM), HEAD_DIM)
        acc = jnp.zeros((HEAD_DIM, HEAD_DIM), jnp.float32)
        for p in range(span // PIECE):
            rows = pl.ds(p * PIECE, PIECE)
            tail = (span - 1.0 - p * PIECE) - lax.broadcasted_iota(
                jnp.int32, (PIECE, HEAD_DIM), 0
            ).astype(jnp.float32)
            kd = k_ref[rows, cols].astype(jnp.float32) * jnp.exp(-rate * tail)
            hi, lo = kernel_split(kd)
            v = v_ref[rows, cols]
            acc = acc + lax.dot_general(hi, v, dims, preferred_element_type=jnp.float32)
            acc = acc + lax.dot_general(lo, v, dims, preferred_element_type=jnp.float32)
        out_ref[hh] = acc
        return carry

    lax.fori_loop(0, GROUP, head, 0)


def block_state(decay_rates, k, v):
    span = k.shape[0]
    groups = HEADS // GROUP
    width = GROUP * HEAD_DIM
    return pl.pallas_call(
        state_kernel,
        grid=(groups,),
        in_specs=[
            pl.BlockSpec(memory_space=pltpu.SMEM),
            pl.BlockSpec((span, width), lambda g: (0, g)),
            pl.BlockSpec((span, width), lambda g: (0, g)),
        ],
        out_specs=pl.BlockSpec((GROUP, HEAD_DIM, HEAD_DIM), lambda g: (g, 0, 0)),
        out_shape=jax.ShapeDtypeStruct((HEADS, HEAD_DIM, HEAD_DIM), jnp.float32),
        cost_estimate=pl.CostEstimate(
            flops=4 * span * HEADS * HEAD_DIM * HEAD_DIM,
            transcendentals=span * HEADS * HEAD_DIM,
            bytes_accessed=2 * 2 * span * HEADS * HEAD_DIM + 4 * HEADS * HEAD_DIM * HEAD_DIM,
        ),
    )(decay_rates, k, v)


def intra_kernel(rates_ref, q_ref, k_ref, v_ref, out_ref):
    g = pl.program_id(0)
    span = q_ref.shape[0]
    rows = lax.broadcasted_iota(jnp.int32, (span, span), 0).astype(jnp.float32)
    cols_i = lax.broadcasted_iota(jnp.int32, (span, span), 1).astype(jnp.float32)
    offsets = rows - cols_i
    causal = offsets >= 0.0
    gap = jnp.maximum(offsets, 0.0)
    for hh in range(GROUP):
        rate = rates_ref[g * GROUP + hh]
        cols = slice(hh * HEAD_DIM, (hh + 1) * HEAD_DIM)
        q = q_ref[:, cols]
        k = k_ref[:, cols]
        scores = lax.dot_general(
            q, k, (((1,), (1,)), ((), ())), preferred_element_type=jnp.float32
        )
        within = jnp.where(causal, jnp.exp(-rate * gap), 0.0)
        weights = (scores * within).astype(jnp.bfloat16)
        out_ref[:, cols] = jnp.dot(weights, v_ref[:, cols], preferred_element_type=jnp.float32)


def block_intra(decay_rates, q, k, v):
    span = q.shape[0]
    groups = HEADS // GROUP
    width = GROUP * HEAD_DIM
    return pl.pallas_call(
        intra_kernel,
        grid=(groups,),
        in_specs=[
            pl.BlockSpec(memory_space=pltpu.SMEM),
            pl.BlockSpec((span, width), lambda g: (0, g)),
            pl.BlockSpec((span, width), lambda g: (0, g)),
            pl.BlockSpec((span, width), lambda g: (0, g)),
        ],
        out_specs=pl.BlockSpec((span, width), lambda g: (0, g)),
        out_shape=jax.ShapeDtypeStruct((span, HEADS * HEAD_DIM), jnp.float32),
        cost_estimate=pl.CostEstimate(
            flops=HEADS * 4 * span * span * HEAD_DIM,
            transcendentals=HEADS * span * span,
            bytes_accessed=3 * 2 * span * HEADS * HEAD_DIM + 4 * span * HEADS * HEAD_DIM,
        ),
    )(decay_rates, q, k, v)


def output_kernel(rates_ref, intra_ref, q_ref, s_ref, gain_ref, out_ref):
    g = pl.program_id(0)
    span = q_ref.shape[0]

    def head(hh, carry):
        rate = rates_ref[g * GROUP + hh]
        cols = pl.ds(pl.multiple_of(hh * HEAD_DIM, HEAD_DIM), HEAD_DIM)
        hi, lo = kernel_split(s_ref[hh])
        gain = gain_ref[pl.ds(hh, 1), :]
        for p in range(span // PIECE):
            rows = pl.ds(p * PIECE, PIECE)
            q = q_ref[rows, cols]
            inter = jnp.dot(q, hi, preferred_element_type=jnp.float32) + jnp.dot(
                q, lo, preferred_element_type=jnp.float32
            )
            lead = lax.broadcasted_iota(jnp.int32, (PIECE, HEAD_DIM), 0).astype(
                jnp.float32
            ) + (p * PIECE + 1.0)
            total = intra_ref[rows, cols] + inter * jnp.exp(-rate * lead)
            mean_square = jnp.mean(total * total, axis=-1, keepdims=True)
            normed = total * lax.rsqrt(mean_square + 1e-06) * gain
            out_ref[rows, cols] = normed.astype(out_ref.dtype)
        return carry

    lax.fori_loop(0, GROUP, head, 0)


def block_output(decay_rates, intra, q, incoming, gains):
    span = q.shape[0]
    groups = HEADS // GROUP
    width = GROUP * HEAD_DIM
    return pl.pallas_call(
        output_kernel,
        grid=(groups,),
        in_specs=[
            pl.BlockSpec(memory_space=pltpu.SMEM),
            pl.BlockSpec((span, width), lambda g: (0, g)),
            pl.BlockSpec((span, width), lambda g: (0, g)),
            pl.BlockSpec((GROUP, HEAD_DIM, HEAD_DIM), lambda g: (g, 0, 0)),
            pl.BlockSpec((GROUP, HEAD_DIM), lambda g: (g, 0)),
        ],
        out_specs=pl.BlockSpec((span, width), lambda g: (0, g)),
        out_shape=jax.ShapeDtypeStruct((span, HEADS * HEAD_DIM), jnp.bfloat16),
        cost_estimate=pl.CostEstimate(
            flops=HEADS * 4 * span * HEAD_DIM * HEAD_DIM,
            transcendentals=HEADS * span,
            bytes_accessed=8 * span * HEADS * HEAD_DIM + 4 * HEADS * HEAD_DIM * HEAD_DIM,
        ),
    )(decay_rates, intra, q, incoming, gains)


def chain_kernel(carry_ref, g_ref, out_ref):
    carry = carry_ref[0]
    state = jnp.zeros(out_ref.shape[1:], jnp.float32)
    out_ref[0] = state

    def step(b, state):
        state = carry * state + g_ref[b - 1]
        out_ref[b] = state
        return state

    lax.fori_loop(1, out_ref.shape[0], step, state, unroll=8)


def block_chain(carry, gathered):
    blocks, rows, width = gathered.shape
    return pl.pallas_call(
        chain_kernel,
        in_specs=[
            pl.BlockSpec(memory_space=pltpu.SMEM),
            pl.BlockSpec(memory_space=pltpu.VMEM),
        ],
        out_specs=pl.BlockSpec(memory_space=pltpu.VMEM),
        out_shape=jax.ShapeDtypeStruct((blocks, rows, width), jnp.float32),
        cost_estimate=pl.CostEstimate(
            flops=2 * blocks * rows * width,
            transcendentals=0,
            bytes_accessed=8 * blocks * rows * width,
        ),
    )(carry, gathered)


def body(n, queries, key_rows, value_rows, decay_rates, norm_gain):
    span = queries.shape[0]
    me = lax.axis_index(AXES)

    local_state = block_state(decay_rates, key_rows, value_rows)

    rows = HEADS * HEAD_DIM // n
    chunks = local_state.reshape(n, rows, HEAD_DIM)
    gathered = lax.all_to_all(chunks, AXES, 0, 0, tiled=True)
    intra = block_intra(decay_rates, queries, key_rows, value_rows)
    head_of_chunk = me // (n // HEADS)
    rate = lax.dynamic_slice_in_dim(decay_rates, head_of_chunk, 1)
    before = block_chain(jnp.exp(-rate * float(span)), gathered)
    incoming = lax.all_to_all(before, AXES, 0, 0, tiled=True)
    incoming = incoming.reshape(HEADS, HEAD_DIM, HEAD_DIM)

    gains = norm_gain.reshape(HEADS, HEAD_DIM)
    return block_output(decay_rates, intra, queries, incoming, gains)


def solution(mesh):
    n = mesh.shape["seq"] * mesh.shape["head"]

    def run(queries, key_rows, value_rows, decay_rates, norm_gain):
        return body(n, queries, key_rows, value_rows, decay_rates, norm_gain)

    return jax.shard_map(
        run,
        mesh=mesh,
        in_specs=(
            P(AXES, None),
            P(AXES, None),
            P(AXES, None),
            P(),
            P(),
        ),
        out_specs=P(AXES, None),
        check_vma=False,
    )
```

```python
import jax
import jax.numpy as jnp
from jax import lax
from jax.experimental import pallas as pl
from jax.experimental.pallas import tpu as pltpu
from jax.sharding import PartitionSpec as P

HEADS = 32
HEAD_DIM = 128
BLOCK = 256
AXES = ("seq", "head")
GROUP = 8
STREAMS = 4


def split_hi_lo(x):
    hi = lax.reduce_precision(x, exponent_bits=8, mantissa_bits=7)
    return hi.astype(jnp.bfloat16), (x - hi).astype(jnp.bfloat16)


def kernel_split(x):
    hi = x.astype(jnp.bfloat16)
    return hi, (x - hi.astype(jnp.float32)).astype(jnp.bfloat16)


def state_kernel(rates_ref, k_ref, v_ref, out_ref):
    g = pl.program_id(0)
    span = k_ref.shape[0]
    tail = (span - 1.0) - lax.broadcasted_iota(jnp.int32, (span, 1), 0).astype(jnp.float32)
    for hh in range(GROUP):
        rate = rates_ref[g * GROUP + hh]
        cols = slice(hh * HEAD_DIM, (hh + 1) * HEAD_DIM)
        kd = k_ref[:, cols].astype(jnp.float32) * jnp.exp(-rate * tail)
        hi, lo = kernel_split(kd)
        v = v_ref[:, cols]
        dims = (((0,), (0,)), ((), ()))
        out_ref[hh] = lax.dot_general(
            hi, v, dims, preferred_element_type=jnp.float32
        ) + lax.dot_general(lo, v, dims, preferred_element_type=jnp.float32)


def block_state(decay_rates, k, v):
    span = k.shape[0]
    groups = HEADS // GROUP
    width = GROUP * HEAD_DIM
    return pl.pallas_call(
        state_kernel,
        grid=(groups,),
        in_specs=[
            pl.BlockSpec(memory_space=pltpu.SMEM),
            pl.BlockSpec((span, width), lambda g: (0, g)),
            pl.BlockSpec((span, width), lambda g: (0, g)),
        ],
        out_specs=pl.BlockSpec((GROUP, HEAD_DIM, HEAD_DIM), lambda g: (g, 0, 0)),
        out_shape=jax.ShapeDtypeStruct((HEADS, HEAD_DIM, HEAD_DIM), jnp.float32),
        cost_estimate=pl.CostEstimate(
            flops=4 * span * HEADS * HEAD_DIM * HEAD_DIM,
            transcendentals=span * HEADS * HEAD_DIM,
            bytes_accessed=2 * 2 * span * HEADS * HEAD_DIM + 4 * HEADS * HEAD_DIM * HEAD_DIM,
        ),
    )(decay_rates, k, v)


def intra_kernel(rates_ref, q_ref, k_ref, v_ref, out_ref):
    g = pl.program_id(0)
    span = q_ref.shape[0]
    rows = lax.broadcasted_iota(jnp.int32, (span, span), 0).astype(jnp.float32)
    cols_i = lax.broadcasted_iota(jnp.int32, (span, span), 1).astype(jnp.float32)
    offsets = rows - cols_i
    causal = offsets >= 0.0
    gap = jnp.maximum(offsets, 0.0)
    for hh in range(GROUP):
        rate = rates_ref[g * GROUP + hh]
        cols = slice(hh * HEAD_DIM, (hh + 1) * HEAD_DIM)
        q = q_ref[:, cols]
        k = k_ref[:, cols]
        scores = lax.dot_general(
            q, k, (((1,), (1,)), ((), ())), preferred_element_type=jnp.float32
        )
        within = jnp.where(causal, jnp.exp(-rate * gap), 0.0)
        weights = (scores * within).astype(jnp.bfloat16)
        out_ref[:, cols] = jnp.dot(weights, v_ref[:, cols], preferred_element_type=jnp.float32)


def block_intra(decay_rates, q, k, v):
    span = q.shape[0]
    groups = HEADS // GROUP
    width = GROUP * HEAD_DIM
    return pl.pallas_call(
        intra_kernel,
        grid=(groups,),
        in_specs=[
            pl.BlockSpec(memory_space=pltpu.SMEM),
            pl.BlockSpec((span, width), lambda g: (0, g)),
            pl.BlockSpec((span, width), lambda g: (0, g)),
            pl.BlockSpec((span, width), lambda g: (0, g)),
        ],
        out_specs=pl.BlockSpec((span, width), lambda g: (0, g)),
        out_shape=jax.ShapeDtypeStruct((span, HEADS * HEAD_DIM), jnp.float32),
        cost_estimate=pl.CostEstimate(
            flops=HEADS * 4 * span * span * HEAD_DIM,
            transcendentals=HEADS * span * span,
            bytes_accessed=3 * 2 * span * HEADS * HEAD_DIM + 4 * span * HEADS * HEAD_DIM,
        ),
    )(decay_rates, q, k, v)


def output_kernel(rates_ref, intra_ref, q_ref, s_ref, gain_ref, out_ref):
    g = pl.program_id(0)
    span = q_ref.shape[0]
    lead = lax.broadcasted_iota(jnp.int32, (span, 1), 0).astype(jnp.float32) + 1.0
    for hh in range(GROUP):
        rate = rates_ref[g * GROUP + hh]
        cols = slice(hh * HEAD_DIM, (hh + 1) * HEAD_DIM)
        q = q_ref[:, cols]
        hi, lo = kernel_split(s_ref[hh])
        inter = jnp.dot(q, hi, preferred_element_type=jnp.float32) + jnp.dot(
            q, lo, preferred_element_type=jnp.float32
        )
        total = intra_ref[:, cols] + inter * jnp.exp(-rate * lead)
        mean_square = jnp.mean(total * total, axis=-1, keepdims=True)
        normed = total * lax.rsqrt(mean_square + 1e-06) * gain_ref[hh : hh + 1, :]
        out_ref[:, cols] = normed.astype(out_ref.dtype)


def block_output(decay_rates, intra, q, incoming, gains):
    span = q.shape[0]
    groups = HEADS // GROUP
    width = GROUP * HEAD_DIM
    return pl.pallas_call(
        output_kernel,
        grid=(groups,),
        in_specs=[
            pl.BlockSpec(memory_space=pltpu.SMEM),
            pl.BlockSpec((span, width), lambda g: (0, g)),
            pl.BlockSpec((span, width), lambda g: (0, g)),
            pl.BlockSpec((GROUP, HEAD_DIM, HEAD_DIM), lambda g: (g, 0, 0)),
            pl.BlockSpec((GROUP, HEAD_DIM), lambda g: (g, 0)),
        ],
        out_specs=pl.BlockSpec((span, width), lambda g: (0, g)),
        out_shape=jax.ShapeDtypeStruct((span, HEADS * HEAD_DIM), jnp.bfloat16),
        cost_estimate=pl.CostEstimate(
            flops=HEADS * 4 * span * HEAD_DIM * HEAD_DIM,
            transcendentals=HEADS * span,
            bytes_accessed=8 * span * HEADS * HEAD_DIM + 4 * HEADS * HEAD_DIM * HEAD_DIM,
        ),
    )(decay_rates, intra, q, incoming, gains)


def chain_kernel(carry_ref, g_hbm, out_hbm, g_vmem, out_vmem, in_sems, out_sems):
    blocks = g_vmem.shape[0]
    size = blocks // STREAMS
    loads = [
        pltpu.make_async_copy(
            g_hbm.at[pl.ds(p * size, size)], g_vmem.at[pl.ds(p * size, size)], in_sems.at[p]
        )
        for p in range(STREAMS)
    ]
    stores = [
        pltpu.make_async_copy(
            out_vmem.at[pl.ds(p * size, size)], out_hbm.at[pl.ds(p * size, size)], out_sems.at[p]
        )
        for p in range(STREAMS)
    ]
    for copy in loads:
        copy.start()
    carry = carry_ref[0]
    state = jnp.zeros(g_vmem.shape[1:], jnp.float32)
    out_vmem[0] = state

    def step(b, state):
        state = carry * state + g_vmem[b - 1]
        out_vmem[b] = state
        return state

    for p in range(STREAMS):
        loads[p].wait()
        first = 1 if p == 0 else p * size
        state = lax.fori_loop(first, (p + 1) * size, step, state, unroll=8)
        stores[p].start()
    for copy in stores:
        copy.wait()


def block_chain(carry, gathered):
    blocks, rows, width = gathered.shape
    return pl.pallas_call(
        chain_kernel,
        in_specs=[
            pl.BlockSpec(memory_space=pltpu.SMEM),
            pl.BlockSpec(memory_space=pl.ANY),
        ],
        out_specs=pl.BlockSpec(memory_space=pl.ANY),
        out_shape=jax.ShapeDtypeStruct((blocks, rows, width), jnp.float32),
        scratch_shapes=[
            pltpu.VMEM((blocks, rows, width), jnp.float32),
            pltpu.VMEM((blocks, rows, width), jnp.float32),
            pltpu.SemaphoreType.DMA((STREAMS,)),
            pltpu.SemaphoreType.DMA((STREAMS,)),
        ],
        cost_estimate=pl.CostEstimate(
            flops=2 * blocks * rows * width,
            transcendentals=0,
            bytes_accessed=8 * blocks * rows * width,
        ),
    )(carry, gathered)


def body(n, queries, key_rows, value_rows, decay_rates, norm_gain):
    span = queries.shape[0]
    me = lax.axis_index(AXES)

    local_state = block_state(decay_rates, key_rows, value_rows)

    rows = HEADS * HEAD_DIM // n
    chunks = local_state.reshape(n, rows, HEAD_DIM)
    gathered = lax.all_to_all(chunks, AXES, 0, 0, tiled=True)
    intra = block_intra(decay_rates, queries, key_rows, value_rows)
    head_of_chunk = me // (n // HEADS)
    rate = lax.dynamic_slice_in_dim(decay_rates, head_of_chunk, 1)
    before = block_chain(jnp.exp(-rate * float(span)), gathered)
    incoming = lax.all_to_all(before, AXES, 0, 0, tiled=True)
    incoming = incoming.reshape(HEADS, HEAD_DIM, HEAD_DIM)

    gains = norm_gain.reshape(HEADS, HEAD_DIM)
    return block_output(decay_rates, intra, queries, incoming, gains)


def solution(mesh):
    n = mesh.shape["seq"] * mesh.shape["head"]

    def run(queries, key_rows, value_rows, decay_rates, norm_gain):
        return body(n, queries, key_rows, value_rows, decay_rates, norm_gain)

    return jax.shard_map(
        run,
        mesh=mesh,
        in_specs=(
            P(AXES, None),
            P(AXES, None),
            P(AXES, None),
            P(),
            P(),
        ),
        out_specs=P(AXES, None),
        check_vma=False,
    )
```

```python
import jax
import jax.numpy as jnp
from jax import lax
from jax.experimental import pallas as pl
from jax.experimental.pallas import tpu as pltpu
from jax.sharding import PartitionSpec as P

HEADS = 32
HEAD_DIM = 128
BLOCK = 256
AXES = ("seq", "head")
GROUP = 8
STREAMS = 4


def split_hi_lo(x):
    hi = lax.reduce_precision(x, exponent_bits=8, mantissa_bits=7)
    return hi.astype(jnp.bfloat16), (x - hi).astype(jnp.bfloat16)


def kernel_split(x):
    hi = x.astype(jnp.bfloat16)
    return hi, (x - hi.astype(jnp.float32)).astype(jnp.bfloat16)


def state_kernel(rates_ref, k_ref, v_ref, out_ref):
    g = pl.program_id(0)
    span = k_ref.shape[0]
    tail = (span - 1.0) - lax.broadcasted_iota(jnp.int32, (span, 1), 0).astype(jnp.float32)
    for hh in range(GROUP):
        rate = rates_ref[g * GROUP + hh]
        cols = slice(hh * HEAD_DIM, (hh + 1) * HEAD_DIM)
        kd = k_ref[:, cols].astype(jnp.float32) * jnp.exp(-rate * tail)
        hi, lo = kernel_split(kd)
        v = v_ref[:, cols]
        dims = (((0,), (0,)), ((), ()))
        out_ref[hh] = lax.dot_general(
            hi, v, dims, preferred_element_type=jnp.float32
        ) + lax.dot_general(lo, v, dims, preferred_element_type=jnp.float32)


def block_state(decay_rates, k, v):
    span = k.shape[0]
    groups = HEADS // GROUP
    width = GROUP * HEAD_DIM
    return pl.pallas_call(
        state_kernel,
        grid=(groups,),
        in_specs=[
            pl.BlockSpec(memory_space=pltpu.SMEM),
            pl.BlockSpec((span, width), lambda g: (0, g)),
            pl.BlockSpec((span, width), lambda g: (0, g)),
        ],
        out_specs=pl.BlockSpec((GROUP, HEAD_DIM, HEAD_DIM), lambda g: (g, 0, 0)),
        out_shape=jax.ShapeDtypeStruct((HEADS, HEAD_DIM, HEAD_DIM), jnp.float32),
        cost_estimate=pl.CostEstimate(
            flops=4 * span * HEADS * HEAD_DIM * HEAD_DIM,
            transcendentals=span * HEADS * HEAD_DIM,
            bytes_accessed=2 * 2 * span * HEADS * HEAD_DIM + 4 * HEADS * HEAD_DIM * HEAD_DIM,
        ),
    )(decay_rates, k, v)


def intra_kernel(rates_ref, q_ref, k_ref, v_ref, out_ref, qhi_ref, qlo_ref):
    g = pl.program_id(0)
    span = q_ref.shape[0]
    rows = lax.broadcasted_iota(jnp.int32, (span, span), 0).astype(jnp.float32)
    cols_i = lax.broadcasted_iota(jnp.int32, (span, span), 1).astype(jnp.float32)
    offsets = rows - cols_i
    causal = offsets >= 0.0
    gap = jnp.maximum(offsets, 0.0)
    lead = lax.broadcasted_iota(jnp.int32, (span, HEAD_DIM), 0).astype(jnp.float32) + 1.0
    for hh in range(GROUP):
        rate = rates_ref[g * GROUP + hh]
        cols = slice(hh * HEAD_DIM, (hh + 1) * HEAD_DIM)
        q = q_ref[:, cols]
        k = k_ref[:, cols]
        scores = lax.dot_general(
            q, k, (((1,), (1,)), ((), ())), preferred_element_type=jnp.float32
        )
        within = jnp.where(causal, jnp.exp(-rate * gap), 0.0)
        weights = (scores * within).astype(jnp.bfloat16)
        out_ref[:, cols] = jnp.dot(weights, v_ref[:, cols], preferred_element_type=jnp.float32)
        q_hi, q_lo = kernel_split(q.astype(jnp.float32) * jnp.exp(-rate * lead))
        qhi_ref[:, cols] = q_hi
        qlo_ref[:, cols] = q_lo


def block_intra(decay_rates, q, k, v):
    span = q.shape[0]
    groups = HEADS // GROUP
    width = GROUP * HEAD_DIM
    tile = pl.BlockSpec((span, width), lambda g: (0, g))
    return pl.pallas_call(
        intra_kernel,
        grid=(groups,),
        in_specs=[pl.BlockSpec(memory_space=pltpu.SMEM), tile, tile, tile],
        out_specs=[tile, tile, tile],
        out_shape=[
            jax.ShapeDtypeStruct((span, HEADS * HEAD_DIM), jnp.float32),
            jax.ShapeDtypeStruct((span, HEADS * HEAD_DIM), jnp.bfloat16),
            jax.ShapeDtypeStruct((span, HEADS * HEAD_DIM), jnp.bfloat16),
        ],
        cost_estimate=pl.CostEstimate(
            flops=HEADS * 4 * span * span * HEAD_DIM,
            transcendentals=HEADS * span * span,
            bytes_accessed=5 * 2 * span * HEADS * HEAD_DIM + 4 * span * HEADS * HEAD_DIM,
        ),
    )(decay_rates, q, k, v)


def output_kernel(intra_ref, qhi_ref, qlo_ref, s_ref, gain_ref, out_ref):
    for hh in range(GROUP):
        cols = slice(hh * HEAD_DIM, (hh + 1) * HEAD_DIM)
        s_hi, s_lo = kernel_split(s_ref[hh])
        q_hi = qhi_ref[:, cols]
        inter = (
            jnp.dot(q_hi, s_hi, preferred_element_type=jnp.float32)
            + jnp.dot(qlo_ref[:, cols], s_hi, preferred_element_type=jnp.float32)
            + jnp.dot(q_hi, s_lo, preferred_element_type=jnp.float32)
        )
        total = intra_ref[:, cols] + inter
        mean_square = jnp.mean(total * total, axis=-1, keepdims=True)
        normed = total * lax.rsqrt(mean_square + 1e-06) * gain_ref[hh : hh + 1, :]
        out_ref[:, cols] = normed.astype(out_ref.dtype)


def block_output(intra, q_hi, q_lo, incoming, gains):
    span = q_hi.shape[0]
    groups = HEADS // GROUP
    width = GROUP * HEAD_DIM
    tile = pl.BlockSpec((span, width), lambda g: (0, g))
    return pl.pallas_call(
        output_kernel,
        grid=(groups,),
        in_specs=[
            tile,
            tile,
            tile,
            pl.BlockSpec((GROUP, HEAD_DIM, HEAD_DIM), lambda g: (g, 0, 0)),
            pl.BlockSpec((GROUP, HEAD_DIM), lambda g: (g, 0)),
        ],
        out_specs=tile,
        out_shape=jax.ShapeDtypeStruct((span, HEADS * HEAD_DIM), jnp.bfloat16),
        cost_estimate=pl.CostEstimate(
            flops=HEADS * 6 * span * HEAD_DIM * HEAD_DIM,
            transcendentals=HEADS * span,
            bytes_accessed=10 * span * HEADS * HEAD_DIM + 4 * HEADS * HEAD_DIM * HEAD_DIM,
        ),
    )(intra, q_hi, q_lo, incoming, gains)


def chain_kernel(carry_ref, g_hbm, out_hbm, g_vmem, out_vmem, in_sems, out_sems):
    blocks = g_vmem.shape[0]
    size = blocks // STREAMS
    loads = [
        pltpu.make_async_copy(
            g_hbm.at[pl.ds(p * size, size)], g_vmem.at[pl.ds(p * size, size)], in_sems.at[p]
        )
        for p in range(STREAMS)
    ]
    stores = [
        pltpu.make_async_copy(
            out_vmem.at[pl.ds(p * size, size)], out_hbm.at[pl.ds(p * size, size)], out_sems.at[p]
        )
        for p in range(STREAMS)
    ]
    for copy in loads:
        copy.start()
    carry = carry_ref[0]
    state = jnp.zeros(g_vmem.shape[1:], jnp.float32)
    out_vmem[0] = state

    def step(b, state):
        state = carry * state + g_vmem[b - 1]
        out_vmem[b] = state
        return state

    for p in range(STREAMS):
        loads[p].wait()
        first = 1 if p == 0 else p * size
        state = lax.fori_loop(first, (p + 1) * size, step, state, unroll=8)
        stores[p].start()
    for copy in stores:
        copy.wait()


def block_chain(carry, gathered):
    blocks, rows, width = gathered.shape
    return pl.pallas_call(
        chain_kernel,
        in_specs=[
            pl.BlockSpec(memory_space=pltpu.SMEM),
            pl.BlockSpec(memory_space=pl.ANY),
        ],
        out_specs=pl.BlockSpec(memory_space=pl.ANY),
        out_shape=jax.ShapeDtypeStruct((blocks, rows, width), jnp.float32),
        scratch_shapes=[
            pltpu.VMEM((blocks, rows, width), jnp.float32),
            pltpu.VMEM((blocks, rows, width), jnp.float32),
            pltpu.SemaphoreType.DMA((STREAMS,)),
            pltpu.SemaphoreType.DMA((STREAMS,)),
        ],
        cost_estimate=pl.CostEstimate(
            flops=2 * blocks * rows * width,
            transcendentals=0,
            bytes_accessed=8 * blocks * rows * width,
        ),
    )(carry, gathered)


def body(n, queries, key_rows, value_rows, decay_rates, norm_gain):
    span = queries.shape[0]
    me = lax.axis_index(AXES)

    local_state = block_state(decay_rates, key_rows, value_rows)

    rows = HEADS * HEAD_DIM // n
    chunks = local_state.reshape(n, rows, HEAD_DIM)
    gathered = lax.all_to_all(chunks, AXES, 0, 0, tiled=True)
    intra, q_hi, q_lo = block_intra(decay_rates, queries, key_rows, value_rows)
    head_of_chunk = me // (n // HEADS)
    rate = lax.dynamic_slice_in_dim(decay_rates, head_of_chunk, 1)
    before = block_chain(jnp.exp(-rate * float(span)), gathered)
    incoming = lax.all_to_all(before, AXES, 0, 0, tiled=True)
    incoming = incoming.reshape(HEADS, HEAD_DIM, HEAD_DIM)

    gains = norm_gain.reshape(HEADS, HEAD_DIM)
    return block_output(intra, q_hi, q_lo, incoming, gains)


def solution(mesh):
    n = mesh.shape["seq"] * mesh.shape["head"]

    def run(queries, key_rows, value_rows, decay_rates, norm_gain):
        return body(n, queries, key_rows, value_rows, decay_rates, norm_gain)

    return jax.shard_map(
        run,
        mesh=mesh,
        in_specs=(
            P(AXES, None),
            P(AXES, None),
            P(AXES, None),
            P(),
            P(),
        ),
        out_specs=P(AXES, None),
        check_vma=False,
    )
```

```python
import jax
import jax.numpy as jnp
from jax import lax
from jax.experimental import pallas as pl
from jax.experimental.pallas import tpu as pltpu
from jax.sharding import PartitionSpec as P

HEADS = 32
HEAD_DIM = 128
BLOCK = 256
AXES = ("seq", "head")
GROUP = 8


def split_hi_lo(x):
    hi = lax.reduce_precision(x, exponent_bits=8, mantissa_bits=7)
    return hi.astype(jnp.bfloat16), (x - hi).astype(jnp.bfloat16)


def kernel_split(x):
    hi = x.astype(jnp.bfloat16)
    return hi, (x - hi.astype(jnp.float32)).astype(jnp.bfloat16)


def state_kernel(rates_ref, k_ref, v_ref, out_ref):
    g = pl.program_id(0)
    span = k_ref.shape[0]
    tail = (span - 1.0) - lax.broadcasted_iota(jnp.int32, (span, 1), 0).astype(jnp.float32)
    for hh in range(GROUP):
        rate = rates_ref[g * GROUP + hh]
        cols = slice(hh * HEAD_DIM, (hh + 1) * HEAD_DIM)
        kd = k_ref[:, cols].astype(jnp.float32) * jnp.exp(-rate * tail)
        hi, lo = kernel_split(kd)
        v = v_ref[:, cols]
        dims = (((0,), (0,)), ((), ()))
        out_ref[hh] = lax.dot_general(
            hi, v, dims, preferred_element_type=jnp.float32
        ) + lax.dot_general(lo, v, dims, preferred_element_type=jnp.float32)


def block_state(decay_rates, k, v):
    span = k.shape[0]
    groups = HEADS // GROUP
    width = GROUP * HEAD_DIM
    return pl.pallas_call(
        state_kernel,
        grid=(groups,),
        in_specs=[
            pl.BlockSpec(memory_space=pltpu.SMEM),
            pl.BlockSpec((span, width), lambda g: (0, g)),
            pl.BlockSpec((span, width), lambda g: (0, g)),
        ],
        out_specs=pl.BlockSpec((GROUP, HEAD_DIM, HEAD_DIM), lambda g: (g, 0, 0)),
        out_shape=jax.ShapeDtypeStruct((HEADS, HEAD_DIM, HEAD_DIM), jnp.float32),
        cost_estimate=pl.CostEstimate(
            flops=4 * span * HEADS * HEAD_DIM * HEAD_DIM,
            transcendentals=span * HEADS * HEAD_DIM,
            bytes_accessed=2 * 2 * span * HEADS * HEAD_DIM + 4 * HEADS * HEAD_DIM * HEAD_DIM,
        ),
    )(decay_rates, k, v)


def intra_kernel(rates_ref, q_ref, k_ref, v_ref, out_ref):
    g = pl.program_id(0)
    span = q_ref.shape[0]
    rows = lax.broadcasted_iota(jnp.int32, (span, span), 0).astype(jnp.float32)
    cols_i = lax.broadcasted_iota(jnp.int32, (span, span), 1).astype(jnp.float32)
    offsets = rows - cols_i
    causal = offsets >= 0.0
    gap = jnp.maximum(offsets, 0.0)
    for hh in range(GROUP):
        rate = rates_ref[g * GROUP + hh]
        cols = slice(hh * HEAD_DIM, (hh + 1) * HEAD_DIM)
        q = q_ref[:, cols]
        k = k_ref[:, cols]
        scores = lax.dot_general(
            q, k, (((1,), (1,)), ((), ())), preferred_element_type=jnp.float32
        )
        within = jnp.where(causal, jnp.exp(-rate * gap), 0.0)
        weights = (scores * within).astype(jnp.bfloat16)
        out_ref[:, cols] = jnp.dot(weights, v_ref[:, cols], preferred_element_type=jnp.float32)


def block_intra(decay_rates, q, k, v):
    span = q.shape[0]
    groups = HEADS // GROUP
    width = GROUP * HEAD_DIM
    return pl.pallas_call(
        intra_kernel,
        grid=(groups,),
        in_specs=[
            pl.BlockSpec(memory_space=pltpu.SMEM),
            pl.BlockSpec((span, width), lambda g: (0, g)),
            pl.BlockSpec((span, width), lambda g: (0, g)),
            pl.BlockSpec((span, width), lambda g: (0, g)),
        ],
        out_specs=pl.BlockSpec((span, width), lambda g: (0, g)),
        out_shape=jax.ShapeDtypeStruct((span, HEADS * HEAD_DIM), jnp.float32),
        cost_estimate=pl.CostEstimate(
            flops=HEADS * 4 * span * span * HEAD_DIM,
            transcendentals=HEADS * span * span,
            bytes_accessed=3 * 2 * span * HEADS * HEAD_DIM + 4 * span * HEADS * HEAD_DIM,
        ),
    )(decay_rates, q, k, v)


def output_kernel(rates_ref, intra_ref, q_ref, s_ref, gain_ref, out_ref):
    g = pl.program_id(0)
    span = q_ref.shape[0]
    lead = lax.broadcasted_iota(jnp.int32, (span, 1), 0).astype(jnp.float32) + 1.0
    for hh in range(GROUP):
        rate = rates_ref[g * GROUP + hh]
        cols = slice(hh * HEAD_DIM, (hh + 1) * HEAD_DIM)
        q = q_ref[:, cols]
        hi, lo = kernel_split(s_ref[g * GROUP + hh])
        inter = jnp.dot(q, hi, preferred_element_type=jnp.float32) + jnp.dot(
            q, lo, preferred_element_type=jnp.float32
        )
        total = intra_ref[:, cols] + inter * jnp.exp(-rate * lead)
        mean_square = jnp.mean(total * total, axis=-1, keepdims=True)
        normed = total * lax.rsqrt(mean_square + 1e-06) * gain_ref[hh : hh + 1, :]
        out_ref[:, cols] = normed.astype(out_ref.dtype)


def block_output(decay_rates, intra, q, incoming, gains):
    span = q.shape[0]
    groups = HEADS // GROUP
    width = GROUP * HEAD_DIM
    return pl.pallas_call(
        output_kernel,
        grid=(groups,),
        in_specs=[
            pl.BlockSpec(memory_space=pltpu.SMEM),
            pl.BlockSpec((span, width), lambda g: (0, g)),
            pl.BlockSpec((span, width), lambda g: (0, g)),
            pl.BlockSpec(memory_space=pltpu.VMEM),
            pl.BlockSpec((GROUP, HEAD_DIM), lambda g: (g, 0)),
        ],
        out_specs=pl.BlockSpec((span, width), lambda g: (0, g)),
        out_shape=jax.ShapeDtypeStruct((span, HEADS * HEAD_DIM), jnp.bfloat16),
        cost_estimate=pl.CostEstimate(
            flops=HEADS * 4 * span * HEAD_DIM * HEAD_DIM,
            transcendentals=HEADS * span,
            bytes_accessed=8 * span * HEADS * HEAD_DIM + 4 * HEADS * HEAD_DIM * HEAD_DIM,
        ),
    )(decay_rates, intra, q, pltpu.with_memory_space_constraint(incoming, pltpu.VMEM), gains)


def chain_kernel(carry_ref, g_ref, out_ref):
    carry = carry_ref[0]
    state = jnp.zeros(out_ref.shape[1:], jnp.float32)
    out_ref[0] = state

    def step(b, state):
        state = carry * state + g_ref[b - 1]
        out_ref[b] = state
        return state

    lax.fori_loop(1, out_ref.shape[0], step, state, unroll=8)


def block_chain(carry, gathered):
    blocks, rows, width = gathered.shape
    return pl.pallas_call(
        chain_kernel,
        in_specs=[
            pl.BlockSpec(memory_space=pltpu.SMEM),
            pl.BlockSpec(memory_space=pltpu.VMEM),
        ],
        out_specs=pl.BlockSpec(memory_space=pltpu.VMEM),
        out_shape=jax.ShapeDtypeStruct((blocks, rows, width), jnp.float32),
        cost_estimate=pl.CostEstimate(
            flops=2 * blocks * rows * width,
            transcendentals=0,
            bytes_accessed=8 * blocks * rows * width,
        ),
    )(carry, pltpu.with_memory_space_constraint(gathered, pltpu.VMEM))


def body(n, queries, key_rows, value_rows, decay_rates, norm_gain):
    span = queries.shape[0]
    me = lax.axis_index(AXES)

    local_state = block_state(decay_rates, key_rows, value_rows)

    rows = HEADS * HEAD_DIM // n
    chunks = local_state.reshape(n, rows, HEAD_DIM)
    gathered = lax.all_to_all(chunks, AXES, 0, 0, tiled=True)
    intra = block_intra(decay_rates, queries, key_rows, value_rows)
    head_of_chunk = me // (n // HEADS)
    rate = lax.dynamic_slice_in_dim(decay_rates, head_of_chunk, 1)
    before = block_chain(jnp.exp(-rate * float(span)), gathered)
    incoming = lax.all_to_all(before, AXES, 0, 0, tiled=True)
    incoming = incoming.reshape(HEADS, HEAD_DIM, HEAD_DIM)

    gains = norm_gain.reshape(HEADS, HEAD_DIM)
    return block_output(decay_rates, intra, queries, incoming, gains)


def solution(mesh):
    n = mesh.shape["seq"] * mesh.shape["head"]

    def run(queries, key_rows, value_rows, decay_rates, norm_gain):
        return body(n, queries, key_rows, value_rows, decay_rates, norm_gain)

    return jax.shard_map(
        run,
        mesh=mesh,
        in_specs=(
            P(AXES, None),
            P(AXES, None),
            P(AXES, None),
            P(),
            P(),
        ),
        out_specs=P(AXES, None),
        check_vma=False,
    )
```

```python
import jax
import jax.numpy as jnp
from jax import lax
from jax.experimental import pallas as pl
from jax.experimental.pallas import tpu as pltpu
from jax.sharding import PartitionSpec as P

HEADS = 32
HEAD_DIM = 128
BLOCK = 256
AXES = ("seq", "head")
GROUP = 4


def split_hi_lo(x):
    hi = lax.reduce_precision(x, exponent_bits=8, mantissa_bits=7)
    return hi.astype(jnp.bfloat16), (x - hi).astype(jnp.bfloat16)


def kernel_split(x):
    hi = x.astype(jnp.bfloat16)
    return hi, (x - hi.astype(jnp.float32)).astype(jnp.bfloat16)


def state_kernel(rates_ref, k_ref, v_ref, out_ref):
    g = pl.program_id(0)
    span = k_ref.shape[0]
    tail = (span - 1.0) - lax.broadcasted_iota(jnp.int32, (span, 1), 0).astype(jnp.float32)
    for hh in range(GROUP):
        rate = rates_ref[g * GROUP + hh]
        cols = slice(hh * HEAD_DIM, (hh + 1) * HEAD_DIM)
        kd = k_ref[:, cols].astype(jnp.float32) * jnp.exp(-rate * tail)
        hi, lo = kernel_split(kd)
        v = v_ref[:, cols]
        dims = (((0,), (0,)), ((), ()))
        out_ref[hh] = lax.dot_general(
            hi, v, dims, preferred_element_type=jnp.float32
        ) + lax.dot_general(lo, v, dims, preferred_element_type=jnp.float32)


def block_state(decay_rates, k, v):
    span = k.shape[0]
    groups = HEADS // GROUP
    width = GROUP * HEAD_DIM
    return pl.pallas_call(
        state_kernel,
        grid=(groups,),
        in_specs=[
            pl.BlockSpec(memory_space=pltpu.SMEM),
            pl.BlockSpec((span, width), lambda g: (0, g)),
            pl.BlockSpec((span, width), lambda g: (0, g)),
        ],
        out_specs=pl.BlockSpec((GROUP, HEAD_DIM, HEAD_DIM), lambda g: (g, 0, 0)),
        out_shape=jax.ShapeDtypeStruct((HEADS, HEAD_DIM, HEAD_DIM), jnp.float32),
        cost_estimate=pl.CostEstimate(
            flops=4 * span * HEADS * HEAD_DIM * HEAD_DIM,
            transcendentals=span * HEADS * HEAD_DIM,
            bytes_accessed=2 * 2 * span * HEADS * HEAD_DIM + 4 * HEADS * HEAD_DIM * HEAD_DIM,
        ),
    )(decay_rates, k, v)


def intra_kernel(rates_ref, q_ref, k_ref, v_ref, out_ref):
    g = pl.program_id(0)
    span = q_ref.shape[0]
    rows = lax.broadcasted_iota(jnp.int32, (span, span), 0).astype(jnp.float32)
    cols_i = lax.broadcasted_iota(jnp.int32, (span, span), 1).astype(jnp.float32)
    offsets = rows - cols_i
    causal = offsets >= 0.0
    gap = jnp.maximum(offsets, 0.0)
    for hh in range(GROUP):
        rate = rates_ref[g * GROUP + hh]
        cols = slice(hh * HEAD_DIM, (hh + 1) * HEAD_DIM)
        q = q_ref[:, cols]
        k = k_ref[:, cols]
        scores = lax.dot_general(
            q, k, (((1,), (1,)), ((), ())), preferred_element_type=jnp.float32
        )
        within = jnp.where(causal, jnp.exp(-rate * gap), 0.0)
        weights = (scores * within).astype(jnp.bfloat16)
        out_ref[:, cols] = jnp.dot(weights, v_ref[:, cols], preferred_element_type=jnp.float32)


def block_intra(decay_rates, q, k, v):
    span = q.shape[0]
    groups = HEADS // GROUP
    width = GROUP * HEAD_DIM
    return pl.pallas_call(
        intra_kernel,
        grid=(groups,),
        in_specs=[
            pl.BlockSpec(memory_space=pltpu.SMEM),
            pl.BlockSpec((span, width), lambda g: (0, g)),
            pl.BlockSpec((span, width), lambda g: (0, g)),
            pl.BlockSpec((span, width), lambda g: (0, g)),
        ],
        out_specs=pl.BlockSpec((span, width), lambda g: (0, g)),
        out_shape=jax.ShapeDtypeStruct((span, HEADS * HEAD_DIM), jnp.float32),
        cost_estimate=pl.CostEstimate(
            flops=HEADS * 4 * span * span * HEAD_DIM,
            transcendentals=HEADS * span * span,
            bytes_accessed=3 * 2 * span * HEADS * HEAD_DIM + 4 * span * HEADS * HEAD_DIM,
        ),
    )(decay_rates, q, k, v)


def output_kernel(rates_ref, intra_ref, q_ref, s_ref, gain_ref, out_ref):
    g = pl.program_id(0)
    span = q_ref.shape[0]
    lead = lax.broadcasted_iota(jnp.int32, (span, 1), 0).astype(jnp.float32) + 1.0
    for hh in range(GROUP):
        rate = rates_ref[g * GROUP + hh]
        cols = slice(hh * HEAD_DIM, (hh + 1) * HEAD_DIM)
        q = q_ref[:, cols]
        hi, lo = kernel_split(s_ref[g * GROUP + hh])
        inter = jnp.dot(q, hi, preferred_element_type=jnp.float32) + jnp.dot(
            q, lo, preferred_element_type=jnp.float32
        )
        total = intra_ref[:, cols] + inter * jnp.exp(-rate * lead)
        mean_square = jnp.mean(total * total, axis=-1, keepdims=True)
        normed = total * lax.rsqrt(mean_square + 1e-06) * gain_ref[pl.ds(g * GROUP + hh, 1), :]
        out_ref[:, cols] = normed.astype(out_ref.dtype)


def block_output(decay_rates, intra, q, incoming, gains):
    span = q.shape[0]
    groups = HEADS // GROUP
    width = GROUP * HEAD_DIM
    return pl.pallas_call(
        output_kernel,
        grid=(groups,),
        in_specs=[
            pl.BlockSpec(memory_space=pltpu.SMEM),
            pl.BlockSpec((span, width), lambda g: (0, g)),
            pl.BlockSpec((span, width), lambda g: (0, g)),
            pl.BlockSpec(memory_space=pltpu.VMEM),
            pl.BlockSpec(memory_space=pltpu.VMEM),
        ],
        out_specs=pl.BlockSpec((span, width), lambda g: (0, g)),
        out_shape=jax.ShapeDtypeStruct((span, HEADS * HEAD_DIM), jnp.bfloat16),
        cost_estimate=pl.CostEstimate(
            flops=HEADS * 4 * span * HEAD_DIM * HEAD_DIM,
            transcendentals=HEADS * span,
            bytes_accessed=8 * span * HEADS * HEAD_DIM + 4 * HEADS * HEAD_DIM * HEAD_DIM,
        ),
    )(decay_rates, intra, q, pltpu.with_memory_space_constraint(incoming, pltpu.VMEM), gains)


def chain_kernel(carry_ref, g_ref, out_ref):
    carry = carry_ref[0]
    state = jnp.zeros(out_ref.shape[1:], jnp.float32)
    out_ref[0] = state

    def step(b, state):
        state = carry * state + g_ref[b - 1]
        out_ref[b] = state
        return state

    lax.fori_loop(1, out_ref.shape[0], step, state, unroll=8)


def block_chain(carry, gathered):
    blocks, rows, width = gathered.shape
    return pl.pallas_call(
        chain_kernel,
        in_specs=[
            pl.BlockSpec(memory_space=pltpu.SMEM),
            pl.BlockSpec(memory_space=pltpu.VMEM),
        ],
        out_specs=pl.BlockSpec(memory_space=pltpu.VMEM),
        out_shape=jax.ShapeDtypeStruct((blocks, rows, width), jnp.float32),
        cost_estimate=pl.CostEstimate(
            flops=2 * blocks * rows * width,
            transcendentals=0,
            bytes_accessed=8 * blocks * rows * width,
        ),
    )(carry, pltpu.with_memory_space_constraint(gathered, pltpu.VMEM))


def body(n, queries, key_rows, value_rows, decay_rates, norm_gain):
    span = queries.shape[0]
    me = lax.axis_index(AXES)

    local_state = block_state(decay_rates, key_rows, value_rows)

    rows = HEADS * HEAD_DIM // n
    chunks = local_state.reshape(n, rows, HEAD_DIM)
    gathered = lax.all_to_all(chunks, AXES, 0, 0, tiled=True)
    intra = block_intra(decay_rates, queries, key_rows, value_rows)
    head_of_chunk = me // (n // HEADS)
    rate = lax.dynamic_slice_in_dim(decay_rates, head_of_chunk, 1)
    before = block_chain(jnp.exp(-rate * float(span)), gathered)
    incoming = lax.all_to_all(before, AXES, 0, 0, tiled=True)
    incoming = incoming.reshape(HEADS, HEAD_DIM, HEAD_DIM)

    gains = norm_gain.reshape(HEADS, HEAD_DIM)
    return block_output(decay_rates, intra, queries, incoming, gains)


def solution(mesh):
    n = mesh.shape["seq"] * mesh.shape["head"]

    def run(queries, key_rows, value_rows, decay_rates, norm_gain):
        return body(n, queries, key_rows, value_rows, decay_rates, norm_gain)

    return jax.shard_map(
        run,
        mesh=mesh,
        in_specs=(
            P(AXES, None),
            P(AXES, None),
            P(AXES, None),
            P(),
            P(),
        ),
        out_specs=P(AXES, None),
        check_vma=False,
    )
```

```python
import jax
import jax.numpy as jnp
from jax import lax
from jax.experimental import pallas as pl
from jax.experimental.pallas import tpu as pltpu
from jax.sharding import PartitionSpec as P

HEADS = 32
HEAD_DIM = 128
BLOCK = 256
AXES = ("seq", "head")
GROUP = 16


def split_hi_lo(x):
    hi = lax.reduce_precision(x, exponent_bits=8, mantissa_bits=7)
    return hi.astype(jnp.bfloat16), (x - hi).astype(jnp.bfloat16)


def kernel_split(x):
    hi = x.astype(jnp.bfloat16)
    return hi, (x - hi.astype(jnp.float32)).astype(jnp.bfloat16)


def state_kernel(rates_ref, k_ref, v_ref, out_ref):
    g = pl.program_id(0)
    span = k_ref.shape[0]
    tail = (span - 1.0) - lax.broadcasted_iota(jnp.int32, (span, 1), 0).astype(jnp.float32)
    for hh in range(GROUP):
        rate = rates_ref[g * GROUP + hh]
        cols = slice(hh * HEAD_DIM, (hh + 1) * HEAD_DIM)
        kd = k_ref[:, cols].astype(jnp.float32) * jnp.exp(-rate * tail)
        hi, lo = kernel_split(kd)
        v = v_ref[:, cols]
        dims = (((0,), (0,)), ((), ()))
        out_ref[hh] = lax.dot_general(
            hi, v, dims, preferred_element_type=jnp.float32
        ) + lax.dot_general(lo, v, dims, preferred_element_type=jnp.float32)


def block_state(decay_rates, k, v):
    span = k.shape[0]
    groups = HEADS // GROUP
    width = GROUP * HEAD_DIM
    return pl.pallas_call(
        state_kernel,
        grid=(groups,),
        in_specs=[
            pl.BlockSpec(memory_space=pltpu.SMEM),
            pl.BlockSpec((span, width), lambda g: (0, g)),
            pl.BlockSpec((span, width), lambda g: (0, g)),
        ],
        out_specs=pl.BlockSpec((GROUP, HEAD_DIM, HEAD_DIM), lambda g: (g, 0, 0)),
        out_shape=jax.ShapeDtypeStruct((HEADS, HEAD_DIM, HEAD_DIM), jnp.float32),
        cost_estimate=pl.CostEstimate(
            flops=4 * span * HEADS * HEAD_DIM * HEAD_DIM,
            transcendentals=span * HEADS * HEAD_DIM,
            bytes_accessed=2 * 2 * span * HEADS * HEAD_DIM + 4 * HEADS * HEAD_DIM * HEAD_DIM,
        ),
    )(decay_rates, k, v)


def intra_kernel(rates_ref, q_ref, k_ref, v_ref, out_ref):
    g = pl.program_id(0)
    span = q_ref.shape[0]
    rows = lax.broadcasted_iota(jnp.int32, (span, span), 0).astype(jnp.float32)
    cols_i = lax.broadcasted_iota(jnp.int32, (span, span), 1).astype(jnp.float32)
    offsets = rows - cols_i
    causal = offsets >= 0.0
    gap = jnp.maximum(offsets, 0.0)
    for hh in range(GROUP):
        rate = rates_ref[g * GROUP + hh]
        cols = slice(hh * HEAD_DIM, (hh + 1) * HEAD_DIM)
        q = q_ref[:, cols]
        k = k_ref[:, cols]
        scores = lax.dot_general(
            q, k, (((1,), (1,)), ((), ())), preferred_element_type=jnp.float32
        )
        within = jnp.where(causal, jnp.exp(-rate * gap), 0.0)
        weights = (scores * within).astype(jnp.bfloat16)
        out_ref[:, cols] = jnp.dot(weights, v_ref[:, cols], preferred_element_type=jnp.float32)


def block_intra(decay_rates, q, k, v):
    span = q.shape[0]
    groups = HEADS // GROUP
    width = GROUP * HEAD_DIM
    return pl.pallas_call(
        intra_kernel,
        grid=(groups,),
        in_specs=[
            pl.BlockSpec(memory_space=pltpu.SMEM),
            pl.BlockSpec((span, width), lambda g: (0, g)),
            pl.BlockSpec((span, width), lambda g: (0, g)),
            pl.BlockSpec((span, width), lambda g: (0, g)),
        ],
        out_specs=pl.BlockSpec((span, width), lambda g: (0, g)),
        out_shape=jax.ShapeDtypeStruct((span, HEADS * HEAD_DIM), jnp.float32),
        cost_estimate=pl.CostEstimate(
            flops=HEADS * 4 * span * span * HEAD_DIM,
            transcendentals=HEADS * span * span,
            bytes_accessed=3 * 2 * span * HEADS * HEAD_DIM + 4 * span * HEADS * HEAD_DIM,
        ),
    )(decay_rates, q, k, v)


def output_kernel(rates_ref, intra_ref, q_ref, s_ref, gain_ref, out_ref):
    g = pl.program_id(0)
    span = q_ref.shape[0]
    lead = lax.broadcasted_iota(jnp.int32, (span, 1), 0).astype(jnp.float32) + 1.0
    for hh in range(GROUP):
        rate = rates_ref[g * GROUP + hh]
        cols = slice(hh * HEAD_DIM, (hh + 1) * HEAD_DIM)
        q = q_ref[:, cols]
        hi, lo = kernel_split(s_ref[g * GROUP + hh])
        inter = jnp.dot(q, hi, preferred_element_type=jnp.float32) + jnp.dot(
            q, lo, preferred_element_type=jnp.float32
        )
        total = intra_ref[:, cols] + inter * jnp.exp(-rate * lead)
        mean_square = jnp.mean(total * total, axis=-1, keepdims=True)
        normed = total * lax.rsqrt(mean_square + 1e-06) * gain_ref[pl.ds(g * GROUP + hh, 1), :]
        out_ref[:, cols] = normed.astype(out_ref.dtype)


def block_output(decay_rates, intra, q, incoming, gains):
    span = q.shape[0]
    groups = HEADS // GROUP
    width = GROUP * HEAD_DIM
    return pl.pallas_call(
        output_kernel,
        grid=(groups,),
        in_specs=[
            pl.BlockSpec(memory_space=pltpu.SMEM),
            pl.BlockSpec((span, width), lambda g: (0, g)),
            pl.BlockSpec((span, width), lambda g: (0, g)),
            pl.BlockSpec(memory_space=pltpu.VMEM),
            pl.BlockSpec(memory_space=pltpu.VMEM),
        ],
        out_specs=pl.BlockSpec((span, width), lambda g: (0, g)),
        out_shape=jax.ShapeDtypeStruct((span, HEADS * HEAD_DIM), jnp.bfloat16),
        cost_estimate=pl.CostEstimate(
            flops=HEADS * 4 * span * HEAD_DIM * HEAD_DIM,
            transcendentals=HEADS * span,
            bytes_accessed=8 * span * HEADS * HEAD_DIM + 4 * HEADS * HEAD_DIM * HEAD_DIM,
        ),
    )(decay_rates, intra, q, pltpu.with_memory_space_constraint(incoming, pltpu.VMEM), gains)


def chain_kernel(carry_ref, g_ref, out_ref):
    carry = carry_ref[0]
    state = jnp.zeros(out_ref.shape[1:], jnp.float32)
    out_ref[0] = state

    def step(b, state):
        state = carry * state + g_ref[b - 1]
        out_ref[b] = state
        return state

    lax.fori_loop(1, out_ref.shape[0], step, state, unroll=8)


def block_chain(carry, gathered):
    blocks, rows, width = gathered.shape
    return pl.pallas_call(
        chain_kernel,
        in_specs=[
            pl.BlockSpec(memory_space=pltpu.SMEM),
            pl.BlockSpec(memory_space=pltpu.VMEM),
        ],
        out_specs=pl.BlockSpec(memory_space=pltpu.VMEM),
        out_shape=jax.ShapeDtypeStruct((blocks, rows, width), jnp.float32),
        cost_estimate=pl.CostEstimate(
            flops=2 * blocks * rows * width,
            transcendentals=0,
            bytes_accessed=8 * blocks * rows * width,
        ),
    )(carry, pltpu.with_memory_space_constraint(gathered, pltpu.VMEM))


def body(n, queries, key_rows, value_rows, decay_rates, norm_gain):
    span = queries.shape[0]
    me = lax.axis_index(AXES)

    local_state = block_state(decay_rates, key_rows, value_rows)

    rows = HEADS * HEAD_DIM // n
    chunks = local_state.reshape(n, rows, HEAD_DIM)
    gathered = lax.all_to_all(chunks, AXES, 0, 0, tiled=True)
    intra = block_intra(decay_rates, queries, key_rows, value_rows)
    head_of_chunk = me // (n // HEADS)
    rate = lax.dynamic_slice_in_dim(decay_rates, head_of_chunk, 1)
    before = block_chain(jnp.exp(-rate * float(span)), gathered)
    incoming = lax.all_to_all(before, AXES, 0, 0, tiled=True)
    incoming = incoming.reshape(HEADS, HEAD_DIM, HEAD_DIM)

    gains = norm_gain.reshape(HEADS, HEAD_DIM)
    return block_output(decay_rates, intra, queries, incoming, gains)


def solution(mesh):
    n = mesh.shape["seq"] * mesh.shape["head"]

    def run(queries, key_rows, value_rows, decay_rates, norm_gain):
        return body(n, queries, key_rows, value_rows, decay_rates, norm_gain)

    return jax.shard_map(
        run,
        mesh=mesh,
        in_specs=(
            P(AXES, None),
            P(AXES, None),
            P(AXES, None),
            P(),
            P(),
        ),
        out_specs=P(AXES, None),
        check_vma=False,
    )
```

```python
import jax
import jax.numpy as jnp
from jax import lax
from jax.experimental import pallas as pl
from jax.experimental.pallas import tpu as pltpu
from jax.sharding import PartitionSpec as P

HEADS = 32
HEAD_DIM = 128
BLOCK = 256
AXES = ("seq", "head")
GROUP = 16
PIECE = 4


def split_hi_lo(x):
    hi = lax.reduce_precision(x, exponent_bits=8, mantissa_bits=7)
    return hi.astype(jnp.bfloat16), (x - hi).astype(jnp.bfloat16)


def kernel_split(x):
    hi = x.astype(jnp.bfloat16)
    return hi, (x - hi.astype(jnp.float32)).astype(jnp.bfloat16)


def column_copies(src, dst, sems, width):
    return [
        pltpu.make_async_copy(
            src.at[:, pl.ds(p * width, width)], dst.at[:, pl.ds(p * width, width)], sems.at[p]
        )
        for p in range(HEADS // PIECE)
    ]


def state_kernel(rates_ref, k_hbm, v_hbm, out_hbm, k_vmem, v_vmem, out_vmem, k_sems, v_sems, out_sems):
    span = k_vmem.shape[0]
    width = PIECE * HEAD_DIM
    k_loads = column_copies(k_hbm, k_vmem, k_sems, width)
    v_loads = column_copies(v_hbm, v_vmem, v_sems, width)
    stores = [
        pltpu.make_async_copy(
            out_vmem.at[pl.ds(p * PIECE, PIECE)], out_hbm.at[pl.ds(p * PIECE, PIECE)], out_sems.at[p]
        )
        for p in range(HEADS // PIECE)
    ]
    for p in range(HEADS // PIECE):
        k_loads[p].start()
        v_loads[p].start()
    tail = (span - 1.0) - lax.broadcasted_iota(jnp.int32, (span, 1), 0).astype(jnp.float32)
    dims = (((0,), (0,)), ((), ()))
    for p in range(HEADS // PIECE):
        k_loads[p].wait()
        v_loads[p].wait()
        for h in range(p * PIECE, (p + 1) * PIECE):
            rate = rates_ref[h]
            cols = slice(h * HEAD_DIM, (h + 1) * HEAD_DIM)
            kd = k_vmem[:, cols].astype(jnp.float32) * jnp.exp(-rate * tail)
            hi, lo = kernel_split(kd)
            v = v_vmem[:, cols]
            out_vmem[h] = lax.dot_general(
                hi, v, dims, preferred_element_type=jnp.float32
            ) + lax.dot_general(lo, v, dims, preferred_element_type=jnp.float32)
        stores[p].start()
    for copy in stores:
        copy.wait()


def block_state(decay_rates, k, v):
    span = k.shape[0]
    pieces = HEADS // PIECE
    return pl.pallas_call(
        state_kernel,
        in_specs=[
            pl.BlockSpec(memory_space=pltpu.SMEM),
            pl.BlockSpec(memory_space=pl.ANY),
            pl.BlockSpec(memory_space=pl.ANY),
        ],
        out_specs=pl.BlockSpec(memory_space=pl.ANY),
        out_shape=jax.ShapeDtypeStruct((HEADS, HEAD_DIM, HEAD_DIM), jnp.float32),
        scratch_shapes=[
            pltpu.VMEM(k.shape, k.dtype),
            pltpu.VMEM(v.shape, v.dtype),
            pltpu.VMEM((HEADS, HEAD_DIM, HEAD_DIM), jnp.float32),
            pltpu.SemaphoreType.DMA((pieces,)),
            pltpu.SemaphoreType.DMA((pieces,)),
            pltpu.SemaphoreType.DMA((pieces,)),
        ],
        cost_estimate=pl.CostEstimate(
            flops=4 * span * HEADS * HEAD_DIM * HEAD_DIM,
            transcendentals=span * HEADS * HEAD_DIM,
            bytes_accessed=2 * 2 * span * HEADS * HEAD_DIM + 4 * HEADS * HEAD_DIM * HEAD_DIM,
        ),
    )(decay_rates, k, v)


def intra_kernel(rates_ref, q_ref, k_ref, v_ref, out_ref):
    g = pl.program_id(0)
    span = q_ref.shape[0]
    rows = lax.broadcasted_iota(jnp.int32, (span, span), 0).astype(jnp.float32)
    cols_i = lax.broadcasted_iota(jnp.int32, (span, span), 1).astype(jnp.float32)
    offsets = rows - cols_i
    causal = offsets >= 0.0
    gap = jnp.maximum(offsets, 0.0)
    for hh in range(GROUP):
        rate = rates_ref[g * GROUP + hh]
        cols = slice(hh * HEAD_DIM, (hh + 1) * HEAD_DIM)
        q = q_ref[:, cols]
        k = k_ref[:, cols]
        scores = lax.dot_general(
            q, k, (((1,), (1,)), ((), ())), preferred_element_type=jnp.float32
        )
        within = jnp.where(causal, jnp.exp(-rate * gap), 0.0)
        weights = (scores * within).astype(jnp.bfloat16)
        out_ref[:, cols] = jnp.dot(weights, v_ref[:, cols], preferred_element_type=jnp.float32)


def block_intra(decay_rates, q, k, v):
    span = q.shape[0]
    groups = HEADS // GROUP
    width = GROUP * HEAD_DIM
    return pl.pallas_call(
        intra_kernel,
        grid=(groups,),
        in_specs=[
            pl.BlockSpec(memory_space=pltpu.SMEM),
            pl.BlockSpec((span, width), lambda g: (0, g)),
            pl.BlockSpec((span, width), lambda g: (0, g)),
            pl.BlockSpec((span, width), lambda g: (0, g)),
        ],
        out_specs=pl.BlockSpec((span, width), lambda g: (0, g)),
        out_shape=jax.ShapeDtypeStruct((span, HEADS * HEAD_DIM), jnp.float32),
        cost_estimate=pl.CostEstimate(
            flops=HEADS * 4 * span * span * HEAD_DIM,
            transcendentals=HEADS * span * span,
            bytes_accessed=3 * 2 * span * HEADS * HEAD_DIM + 4 * span * HEADS * HEAD_DIM,
        ),
    )(decay_rates, q, k, v)


def output_kernel(
    rates_ref, intra_hbm, q_hbm, s_ref, gain_ref, out_hbm, intra_vmem, q_vmem, out_vmem, i_sems, q_sems, o_sems
):
    span = q_vmem.shape[0]
    width = PIECE * HEAD_DIM
    i_loads = column_copies(intra_hbm, intra_vmem, i_sems, width)
    q_loads = column_copies(q_hbm, q_vmem, q_sems, width)
    stores = column_copies(out_vmem, out_hbm, o_sems, width)
    for p in range(HEADS // PIECE):
        i_loads[p].start()
        q_loads[p].start()
    lead = lax.broadcasted_iota(jnp.int32, (span, 1), 0).astype(jnp.float32) + 1.0
    for p in range(HEADS // PIECE):
        i_loads[p].wait()
        q_loads[p].wait()
        for h in range(p * PIECE, (p + 1) * PIECE):
            rate = rates_ref[h]
            cols = slice(h * HEAD_DIM, (h + 1) * HEAD_DIM)
            q = q_vmem[:, cols]
            hi, lo = kernel_split(s_ref[h])
            inter = jnp.dot(q, hi, preferred_element_type=jnp.float32) + jnp.dot(
                q, lo, preferred_element_type=jnp.float32
            )
            total = intra_vmem[:, cols] + inter * jnp.exp(-rate * lead)
            mean_square = jnp.mean(total * total, axis=-1, keepdims=True)
            normed = total * lax.rsqrt(mean_square + 1e-06) * gain_ref[h : h + 1, :]
            out_vmem[:, cols] = normed.astype(out_vmem.dtype)
        stores[p].start()
    for copy in stores:
        copy.wait()


def block_output(decay_rates, intra, q, incoming, gains):
    span = q.shape[0]
    pieces = HEADS // PIECE
    return pl.pallas_call(
        output_kernel,
        in_specs=[
            pl.BlockSpec(memory_space=pltpu.SMEM),
            pl.BlockSpec(memory_space=pl.ANY),
            pl.BlockSpec(memory_space=pl.ANY),
            pl.BlockSpec(memory_space=pltpu.VMEM),
            pl.BlockSpec(memory_space=pltpu.VMEM),
        ],
        out_specs=pl.BlockSpec(memory_space=pl.ANY),
        out_shape=jax.ShapeDtypeStruct((span, HEADS * HEAD_DIM), jnp.bfloat16),
        scratch_shapes=[
            pltpu.VMEM(intra.shape, intra.dtype),
            pltpu.VMEM(q.shape, q.dtype),
            pltpu.VMEM((span, HEADS * HEAD_DIM), jnp.bfloat16),
            pltpu.SemaphoreType.DMA((pieces,)),
            pltpu.SemaphoreType.DMA((pieces,)),
            pltpu.SemaphoreType.DMA((pieces,)),
        ],
        cost_estimate=pl.CostEstimate(
            flops=HEADS * 4 * span * HEAD_DIM * HEAD_DIM,
            transcendentals=HEADS * span,
            bytes_accessed=8 * span * HEADS * HEAD_DIM + 4 * HEADS * HEAD_DIM * HEAD_DIM,
        ),
    )(decay_rates, intra, q, pltpu.with_memory_space_constraint(incoming, pltpu.VMEM), gains)


def chain_kernel(carry_ref, g_ref, out_ref):
    carry = carry_ref[0]
    state = jnp.zeros(out_ref.shape[1:], jnp.float32)
    out_ref[0] = state

    def step(b, state):
        state = carry * state + g_ref[b - 1]
        out_ref[b] = state
        return state

    lax.fori_loop(1, out_ref.shape[0], step, state, unroll=8)


def block_chain(carry, gathered):
    blocks, rows, width = gathered.shape
    return pl.pallas_call(
        chain_kernel,
        in_specs=[
            pl.BlockSpec(memory_space=pltpu.SMEM),
            pl.BlockSpec(memory_space=pltpu.VMEM),
        ],
        out_specs=pl.BlockSpec(memory_space=pltpu.VMEM),
        out_shape=jax.ShapeDtypeStruct((blocks, rows, width), jnp.float32),
        cost_estimate=pl.CostEstimate(
            flops=2 * blocks * rows * width,
            transcendentals=0,
            bytes_accessed=8 * blocks * rows * width,
        ),
    )(carry, pltpu.with_memory_space_constraint(gathered, pltpu.VMEM))


def body(n, queries, key_rows, value_rows, decay_rates, norm_gain):
    span = queries.shape[0]
    me = lax.axis_index(AXES)

    local_state = block_state(decay_rates, key_rows, value_rows)

    rows = HEADS * HEAD_DIM // n
    chunks = local_state.reshape(n, rows, HEAD_DIM)
    gathered = lax.all_to_all(chunks, AXES, 0, 0, tiled=True)
    intra = block_intra(decay_rates, queries, key_rows, value_rows)
    head_of_chunk = me // (n // HEADS)
    rate = lax.dynamic_slice_in_dim(decay_rates, head_of_chunk, 1)
    before = block_chain(jnp.exp(-rate * float(span)), gathered)
    incoming = lax.all_to_all(before, AXES, 0, 0, tiled=True)
    incoming = incoming.reshape(HEADS, HEAD_DIM, HEAD_DIM)

    gains = norm_gain.reshape(HEADS, HEAD_DIM)
    return block_output(decay_rates, intra, queries, incoming, gains)


def solution(mesh):
    n = mesh.shape["seq"] * mesh.shape["head"]

    def run(queries, key_rows, value_rows, decay_rates, norm_gain):
        return body(n, queries, key_rows, value_rows, decay_rates, norm_gain)

    return jax.shard_map(
        run,
        mesh=mesh,
        in_specs=(
            P(AXES, None),
            P(AXES, None),
            P(AXES, None),
            P(),
            P(),
        ),
        out_specs=P(AXES, None),
        check_vma=False,
    )
```

```python
import jax
import jax.numpy as jnp
from jax import lax
from jax.experimental import pallas as pl
from jax.experimental.pallas import tpu as pltpu
from jax.sharding import PartitionSpec as P

HEADS = 32
HEAD_DIM = 128
BLOCK = 256
AXES = ("seq", "head")
GROUP = 16
STREAMS = 4


def split_hi_lo(x):
    hi = lax.reduce_precision(x, exponent_bits=8, mantissa_bits=7)
    return hi.astype(jnp.bfloat16), (x - hi).astype(jnp.bfloat16)


def kernel_split(x):
    hi = x.astype(jnp.bfloat16)
    return hi, (x - hi.astype(jnp.float32)).astype(jnp.bfloat16)


def state_kernel(rates_ref, k_ref, v_ref, out_ref):
    g = pl.program_id(0)
    span = k_ref.shape[0]
    tail = (span - 1.0) - lax.broadcasted_iota(jnp.int32, (span, 1), 0).astype(jnp.float32)
    for hh in range(GROUP):
        rate = rates_ref[g * GROUP + hh]
        cols = slice(hh * HEAD_DIM, (hh + 1) * HEAD_DIM)
        kd = k_ref[:, cols].astype(jnp.float32) * jnp.exp(-rate * tail)
        hi, lo = kernel_split(kd)
        v = v_ref[:, cols]
        dims = (((0,), (0,)), ((), ()))
        out_ref[hh] = lax.dot_general(
            hi, v, dims, preferred_element_type=jnp.float32
        ) + lax.dot_general(lo, v, dims, preferred_element_type=jnp.float32)


def block_state(decay_rates, k, v):
    span = k.shape[0]
    groups = HEADS // GROUP
    width = GROUP * HEAD_DIM
    return pl.pallas_call(
        state_kernel,
        grid=(groups,),
        in_specs=[
            pl.BlockSpec(memory_space=pltpu.SMEM),
            pl.BlockSpec((span, width), lambda g: (0, g)),
            pl.BlockSpec((span, width), lambda g: (0, g)),
        ],
        out_specs=pl.BlockSpec((GROUP, HEAD_DIM, HEAD_DIM), lambda g: (g, 0, 0)),
        out_shape=jax.ShapeDtypeStruct((HEADS, HEAD_DIM, HEAD_DIM), jnp.float32),
        cost_estimate=pl.CostEstimate(
            flops=4 * span * HEADS * HEAD_DIM * HEAD_DIM,
            transcendentals=span * HEADS * HEAD_DIM,
            bytes_accessed=2 * 2 * span * HEADS * HEAD_DIM + 4 * HEADS * HEAD_DIM * HEAD_DIM,
        ),
    )(decay_rates, k, v)


def intra_kernel(rates_ref, q_ref, k_ref, v_ref, out_ref):
    g = pl.program_id(0)
    span = q_ref.shape[0]
    rows = lax.broadcasted_iota(jnp.int32, (span, span), 0).astype(jnp.float32)
    cols_i = lax.broadcasted_iota(jnp.int32, (span, span), 1).astype(jnp.float32)
    offsets = rows - cols_i
    causal = offsets >= 0.0
    gap = jnp.maximum(offsets, 0.0)
    for hh in range(GROUP):
        rate = rates_ref[g * GROUP + hh]
        cols = slice(hh * HEAD_DIM, (hh + 1) * HEAD_DIM)
        q = q_ref[:, cols]
        k = k_ref[:, cols]
        scores = lax.dot_general(
            q, k, (((1,), (1,)), ((), ())), preferred_element_type=jnp.float32
        )
        within = jnp.where(causal, jnp.exp(-rate * gap), 0.0)
        weights = (scores * within).astype(jnp.bfloat16)
        out_ref[:, cols] = jnp.dot(weights, v_ref[:, cols], preferred_element_type=jnp.float32)


def block_intra(decay_rates, q, k, v):
    span = q.shape[0]
    groups = HEADS // GROUP
    width = GROUP * HEAD_DIM
    return pl.pallas_call(
        intra_kernel,
        grid=(groups,),
        in_specs=[
            pl.BlockSpec(memory_space=pltpu.SMEM),
            pl.BlockSpec((span, width), lambda g: (0, g)),
            pl.BlockSpec((span, width), lambda g: (0, g)),
            pl.BlockSpec((span, width), lambda g: (0, g)),
        ],
        out_specs=pl.BlockSpec((span, width), lambda g: (0, g)),
        out_shape=jax.ShapeDtypeStruct((span, HEADS * HEAD_DIM), jnp.float32),
        cost_estimate=pl.CostEstimate(
            flops=HEADS * 4 * span * span * HEAD_DIM,
            transcendentals=HEADS * span * span,
            bytes_accessed=3 * 2 * span * HEADS * HEAD_DIM + 4 * span * HEADS * HEAD_DIM,
        ),
    )(decay_rates, q, k, v)


def output_kernel(rates_ref, intra_ref, q_ref, s_ref, gain_ref, out_ref):
    g = pl.program_id(0)
    span = q_ref.shape[0]
    lead = lax.broadcasted_iota(jnp.int32, (span, 1), 0).astype(jnp.float32) + 1.0
    for hh in range(GROUP):
        rate = rates_ref[g * GROUP + hh]
        cols = slice(hh * HEAD_DIM, (hh + 1) * HEAD_DIM)
        q = q_ref[:, cols]
        hi, lo = kernel_split(s_ref[g * GROUP + hh])
        inter = jnp.dot(q, hi, preferred_element_type=jnp.float32) + jnp.dot(
            q, lo, preferred_element_type=jnp.float32
        )
        total = intra_ref[:, cols] + inter * jnp.exp(-rate * lead)
        mean_square = jnp.mean(total * total, axis=-1, keepdims=True)
        normed = total * lax.rsqrt(mean_square + 1e-06) * gain_ref[pl.ds(g * GROUP + hh, 1), :]
        out_ref[:, cols] = normed.astype(out_ref.dtype)


def block_output(decay_rates, intra, q, incoming, gains):
    span = q.shape[0]
    groups = HEADS // GROUP
    width = GROUP * HEAD_DIM
    return pl.pallas_call(
        output_kernel,
        grid=(groups,),
        in_specs=[
            pl.BlockSpec(memory_space=pltpu.SMEM),
            pl.BlockSpec((span, width), lambda g: (0, g)),
            pl.BlockSpec((span, width), lambda g: (0, g)),
            pl.BlockSpec(memory_space=pltpu.VMEM),
            pl.BlockSpec(memory_space=pltpu.VMEM),
        ],
        out_specs=pl.BlockSpec((span, width), lambda g: (0, g)),
        out_shape=jax.ShapeDtypeStruct((span, HEADS * HEAD_DIM), jnp.bfloat16),
        cost_estimate=pl.CostEstimate(
            flops=HEADS * 4 * span * HEAD_DIM * HEAD_DIM,
            transcendentals=HEADS * span,
            bytes_accessed=8 * span * HEADS * HEAD_DIM + 4 * HEADS * HEAD_DIM * HEAD_DIM,
        ),
    )(decay_rates, intra, q, pltpu.with_memory_space_constraint(incoming, pltpu.VMEM), gains)


def chain_kernel(carry_ref, g_ref, out_hbm, out_vmem, out_sems):
    blocks = g_ref.shape[0]
    size = blocks // STREAMS
    stores = [
        pltpu.make_async_copy(
            out_vmem.at[pl.ds(p * size, size)], out_hbm.at[pl.ds(p * size, size)], out_sems.at[p]
        )
        for p in range(STREAMS)
    ]
    carry = carry_ref[0]
    state = jnp.zeros(g_ref.shape[1:], jnp.float32)
    out_vmem[0] = state

    def step(b, state):
        state = carry * state + g_ref[b - 1]
        out_vmem[b] = state
        return state

    for p in range(STREAMS):
        first = 1 if p == 0 else p * size
        state = lax.fori_loop(first, (p + 1) * size, step, state, unroll=8)
        stores[p].start()
    for copy in stores:
        copy.wait()


def block_chain(carry, gathered):
    blocks, rows, width = gathered.shape
    return pl.pallas_call(
        chain_kernel,
        in_specs=[
            pl.BlockSpec(memory_space=pltpu.SMEM),
            pl.BlockSpec(memory_space=pltpu.VMEM),
        ],
        out_specs=pl.BlockSpec(memory_space=pl.ANY),
        out_shape=jax.ShapeDtypeStruct((blocks, rows, width), jnp.float32),
        scratch_shapes=[
            pltpu.VMEM((blocks, rows, width), jnp.float32),
            pltpu.SemaphoreType.DMA((STREAMS,)),
        ],
        cost_estimate=pl.CostEstimate(
            flops=2 * blocks * rows * width,
            transcendentals=0,
            bytes_accessed=8 * blocks * rows * width,
        ),
    )(carry, pltpu.with_memory_space_constraint(gathered, pltpu.VMEM))


def body(n, queries, key_rows, value_rows, decay_rates, norm_gain):
    span = queries.shape[0]
    me = lax.axis_index(AXES)

    local_state = block_state(decay_rates, key_rows, value_rows)

    rows = HEADS * HEAD_DIM // n
    chunks = local_state.reshape(n, rows, HEAD_DIM)
    gathered = lax.all_to_all(chunks, AXES, 0, 0, tiled=True)
    intra = block_intra(decay_rates, queries, key_rows, value_rows)
    head_of_chunk = me // (n // HEADS)
    rate = lax.dynamic_slice_in_dim(decay_rates, head_of_chunk, 1)
    before = block_chain(jnp.exp(-rate * float(span)), gathered)
    incoming = lax.all_to_all(before, AXES, 0, 0, tiled=True)
    incoming = incoming.reshape(HEADS, HEAD_DIM, HEAD_DIM)

    gains = norm_gain.reshape(HEADS, HEAD_DIM)
    return block_output(decay_rates, intra, queries, incoming, gains)


def solution(mesh):
    n = mesh.shape["seq"] * mesh.shape["head"]

    def run(queries, key_rows, value_rows, decay_rates, norm_gain):
        return body(n, queries, key_rows, value_rows, decay_rates, norm_gain)

    return jax.shard_map(
        run,
        mesh=mesh,
        in_specs=(
            P(AXES, None),
            P(AXES, None),
            P(AXES, None),
            P(),
            P(),
        ),
        out_specs=P(AXES, None),
        check_vma=False,
    )
```

```python
import jax
import jax.numpy as jnp
from jax import lax
from jax.experimental import pallas as pl
from jax.experimental.pallas import tpu as pltpu
from jax.sharding import PartitionSpec as P

HEADS = 32
HEAD_DIM = 128
BLOCK = 256
AXES = ("seq", "head")
GROUP = 16
PIECE = 16
STREAMS = 4


def split_hi_lo(x):
    hi = lax.reduce_precision(x, exponent_bits=8, mantissa_bits=7)
    return hi.astype(jnp.bfloat16), (x - hi).astype(jnp.bfloat16)


def kernel_split(x):
    hi = x.astype(jnp.bfloat16)
    return hi, (x - hi.astype(jnp.float32)).astype(jnp.bfloat16)


def column_copies(src, dst, sems, width):
    return [
        pltpu.make_async_copy(
            src.at[:, pl.ds(p * width, width)], dst.at[:, pl.ds(p * width, width)], sems.at[p]
        )
        for p in range(HEADS // PIECE)
    ]


def state_kernel(rates_ref, k_hbm, v_hbm, out_hbm, k_vmem, v_vmem, out_vmem, k_sems, v_sems, out_sems):
    span = k_vmem.shape[0]
    width = PIECE * HEAD_DIM
    k_loads = column_copies(k_hbm, k_vmem, k_sems, width)
    v_loads = column_copies(v_hbm, v_vmem, v_sems, width)
    stores = [
        pltpu.make_async_copy(
            out_vmem.at[pl.ds(p * PIECE, PIECE)], out_hbm.at[pl.ds(p * PIECE, PIECE)], out_sems.at[p]
        )
        for p in range(HEADS // PIECE)
    ]
    for p in range(HEADS // PIECE):
        k_loads[p].start()
        v_loads[p].start()
    tail = (span - 1.0) - lax.broadcasted_iota(jnp.int32, (span, 1), 0).astype(jnp.float32)
    dims = (((0,), (0,)), ((), ()))
    for p in range(HEADS // PIECE):
        k_loads[p].wait()
        v_loads[p].wait()
        for h in range(p * PIECE, (p + 1) * PIECE):
            rate = rates_ref[h]
            cols = slice(h * HEAD_DIM, (h + 1) * HEAD_DIM)
            kd = k_vmem[:, cols].astype(jnp.float32) * jnp.exp(-rate * tail)
            hi, lo = kernel_split(kd)
            v = v_vmem[:, cols]
            out_vmem[h] = lax.dot_general(
                hi, v, dims, preferred_element_type=jnp.float32
            ) + lax.dot_general(lo, v, dims, preferred_element_type=jnp.float32)
        stores[p].start()
    for copy in stores:
        copy.wait()


def block_state(decay_rates, k, v):
    span = k.shape[0]
    pieces = HEADS // PIECE
    return pl.pallas_call(
        state_kernel,
        in_specs=[
            pl.BlockSpec(memory_space=pltpu.SMEM),
            pl.BlockSpec(memory_space=pl.ANY),
            pl.BlockSpec(memory_space=pl.ANY),
        ],
        out_specs=pl.BlockSpec(memory_space=pl.ANY),
        out_shape=jax.ShapeDtypeStruct((HEADS, HEAD_DIM, HEAD_DIM), jnp.float32),
        scratch_shapes=[
            pltpu.VMEM(k.shape, k.dtype),
            pltpu.VMEM(v.shape, v.dtype),
            pltpu.VMEM((HEADS, HEAD_DIM, HEAD_DIM), jnp.float32),
            pltpu.SemaphoreType.DMA((pieces,)),
            pltpu.SemaphoreType.DMA((pieces,)),
            pltpu.SemaphoreType.DMA((pieces,)),
        ],
        cost_estimate=pl.CostEstimate(
            flops=4 * span * HEADS * HEAD_DIM * HEAD_DIM,
            transcendentals=span * HEADS * HEAD_DIM,
            bytes_accessed=2 * 2 * span * HEADS * HEAD_DIM + 4 * HEADS * HEAD_DIM * HEAD_DIM,
        ),
    )(decay_rates, k, v)


def intra_kernel(rates_ref, q_ref, k_ref, v_ref, out_ref):
    g = pl.program_id(0)
    span = q_ref.shape[0]
    rows = lax.broadcasted_iota(jnp.int32, (span, span), 0).astype(jnp.float32)
    cols_i = lax.broadcasted_iota(jnp.int32, (span, span), 1).astype(jnp.float32)
    offsets = rows - cols_i
    causal = offsets >= 0.0
    gap = jnp.maximum(offsets, 0.0)
    for hh in range(GROUP):
        rate = rates_ref[g * GROUP + hh]
        cols = slice(hh * HEAD_DIM, (hh + 1) * HEAD_DIM)
        q = q_ref[:, cols]
        k = k_ref[:, cols]
        scores = lax.dot_general(
            q, k, (((1,), (1,)), ((), ())), preferred_element_type=jnp.float32
        )
        within = jnp.where(causal, jnp.exp(-rate * gap), 0.0)
        weights = (scores * within).astype(jnp.bfloat16)
        out_ref[:, cols] = jnp.dot(weights, v_ref[:, cols], preferred_element_type=jnp.float32)


def block_intra(decay_rates, q, k, v):
    span = q.shape[0]
    groups = HEADS // GROUP
    width = GROUP * HEAD_DIM
    return pl.pallas_call(
        intra_kernel,
        grid=(groups,),
        in_specs=[
            pl.BlockSpec(memory_space=pltpu.SMEM),
            pl.BlockSpec((span, width), lambda g: (0, g)),
            pl.BlockSpec((span, width), lambda g: (0, g)),
            pl.BlockSpec((span, width), lambda g: (0, g)),
        ],
        out_specs=pl.BlockSpec((span, width), lambda g: (0, g)),
        out_shape=jax.ShapeDtypeStruct((span, HEADS * HEAD_DIM), jnp.float32),
        cost_estimate=pl.CostEstimate(
            flops=HEADS * 4 * span * span * HEAD_DIM,
            transcendentals=HEADS * span * span,
            bytes_accessed=3 * 2 * span * HEADS * HEAD_DIM + 4 * span * HEADS * HEAD_DIM,
        ),
    )(decay_rates, q, k, v)


def output_kernel(
    rates_ref, intra_hbm, q_hbm, s_ref, gain_ref, out_hbm, intra_vmem, q_vmem, out_vmem, i_sems, q_sems, o_sems
):
    span = q_vmem.shape[0]
    width = PIECE * HEAD_DIM
    i_loads = column_copies(intra_hbm, intra_vmem, i_sems, width)
    q_loads = column_copies(q_hbm, q_vmem, q_sems, width)
    stores = column_copies(out_vmem, out_hbm, o_sems, width)
    for p in range(HEADS // PIECE):
        i_loads[p].start()
        q_loads[p].start()
    lead = lax.broadcasted_iota(jnp.int32, (span, 1), 0).astype(jnp.float32) + 1.0
    for p in range(HEADS // PIECE):
        i_loads[p].wait()
        q_loads[p].wait()
        for h in range(p * PIECE, (p + 1) * PIECE):
            rate = rates_ref[h]
            cols = slice(h * HEAD_DIM, (h + 1) * HEAD_DIM)
            q = q_vmem[:, cols]
            hi, lo = kernel_split(s_ref[h])
            inter = jnp.dot(q, hi, preferred_element_type=jnp.float32) + jnp.dot(
                q, lo, preferred_element_type=jnp.float32
            )
            total = intra_vmem[:, cols] + inter * jnp.exp(-rate * lead)
            mean_square = jnp.mean(total * total, axis=-1, keepdims=True)
            normed = total * lax.rsqrt(mean_square + 1e-06) * gain_ref[h : h + 1, :]
            out_vmem[:, cols] = normed.astype(out_vmem.dtype)
        stores[p].start()
    for copy in stores:
        copy.wait()


def block_output(decay_rates, intra, q, incoming, gains):
    span = q.shape[0]
    pieces = HEADS // PIECE
    return pl.pallas_call(
        output_kernel,
        in_specs=[
            pl.BlockSpec(memory_space=pltpu.SMEM),
            pl.BlockSpec(memory_space=pl.ANY),
            pl.BlockSpec(memory_space=pl.ANY),
            pl.BlockSpec(memory_space=pltpu.VMEM),
            pl.BlockSpec(memory_space=pltpu.VMEM),
        ],
        out_specs=pl.BlockSpec(memory_space=pl.ANY),
        out_shape=jax.ShapeDtypeStruct((span, HEADS * HEAD_DIM), jnp.bfloat16),
        scratch_shapes=[
            pltpu.VMEM(intra.shape, intra.dtype),
            pltpu.VMEM(q.shape, q.dtype),
            pltpu.VMEM((span, HEADS * HEAD_DIM), jnp.bfloat16),
            pltpu.SemaphoreType.DMA((pieces,)),
            pltpu.SemaphoreType.DMA((pieces,)),
            pltpu.SemaphoreType.DMA((pieces,)),
        ],
        cost_estimate=pl.CostEstimate(
            flops=HEADS * 4 * span * HEAD_DIM * HEAD_DIM,
            transcendentals=HEADS * span,
            bytes_accessed=8 * span * HEADS * HEAD_DIM + 4 * HEADS * HEAD_DIM * HEAD_DIM,
        ),
    )(decay_rates, intra, q, pltpu.with_memory_space_constraint(incoming, pltpu.VMEM), gains)


def chain_kernel(carry_ref, g_ref, out_hbm, out_vmem, out_sems):
    blocks = g_ref.shape[0]
    size = blocks // STREAMS
    stores = [
        pltpu.make_async_copy(
            out_vmem.at[pl.ds(p * size, size)], out_hbm.at[pl.ds(p * size, size)], out_sems.at[p]
        )
        for p in range(STREAMS)
    ]
    carry = carry_ref[0]
    state = jnp.zeros(g_ref.shape[1:], jnp.float32)
    out_vmem[0] = state

    def step(b, state):
        state = carry * state + g_ref[b - 1]
        out_vmem[b] = state
        return state

    for p in range(STREAMS):
        first = 1 if p == 0 else p * size
        state = lax.fori_loop(first, (p + 1) * size, step, state, unroll=8)
        stores[p].start()
    for copy in stores:
        copy.wait()


def block_chain(carry, gathered):
    blocks, rows, width = gathered.shape
    return pl.pallas_call(
        chain_kernel,
        in_specs=[
            pl.BlockSpec(memory_space=pltpu.SMEM),
            pl.BlockSpec(memory_space=pltpu.VMEM),
        ],
        out_specs=pl.BlockSpec(memory_space=pl.ANY),
        out_shape=jax.ShapeDtypeStruct((blocks, rows, width), jnp.float32),
        scratch_shapes=[
            pltpu.VMEM((blocks, rows, width), jnp.float32),
            pltpu.SemaphoreType.DMA((STREAMS,)),
        ],
        cost_estimate=pl.CostEstimate(
            flops=2 * blocks * rows * width,
            transcendentals=0,
            bytes_accessed=8 * blocks * rows * width,
        ),
    )(carry, pltpu.with_memory_space_constraint(gathered, pltpu.VMEM))


def body(n, queries, key_rows, value_rows, decay_rates, norm_gain):
    span = queries.shape[0]
    me = lax.axis_index(AXES)

    local_state = block_state(decay_rates, key_rows, value_rows)

    rows = HEADS * HEAD_DIM // n
    chunks = local_state.reshape(n, rows, HEAD_DIM)
    gathered = lax.all_to_all(chunks, AXES, 0, 0, tiled=True)
    intra = block_intra(decay_rates, queries, key_rows, value_rows)
    head_of_chunk = me // (n // HEADS)
    rate = lax.dynamic_slice_in_dim(decay_rates, head_of_chunk, 1)
    before = block_chain(jnp.exp(-rate * float(span)), gathered)
    incoming = lax.all_to_all(before, AXES, 0, 0, tiled=True)
    incoming = incoming.reshape(HEADS, HEAD_DIM, HEAD_DIM)

    gains = norm_gain.reshape(HEADS, HEAD_DIM)
    return block_output(decay_rates, intra, queries, incoming, gains)


def solution(mesh):
    n = mesh.shape["seq"] * mesh.shape["head"]

    def run(queries, key_rows, value_rows, decay_rates, norm_gain):
        return body(n, queries, key_rows, value_rows, decay_rates, norm_gain)

    return jax.shard_map(
        run,
        mesh=mesh,
        in_specs=(
            P(AXES, None),
            P(AXES, None),
            P(AXES, None),
            P(),
            P(),
        ),
        out_specs=P(AXES, None),
        check_vma=False,
    )
```

```python
import jax
import jax.numpy as jnp
from jax import lax
from jax.experimental import pallas as pl
from jax.experimental.pallas import tpu as pltpu
from jax.sharding import PartitionSpec as P

HEADS = 32
HEAD_DIM = 128
BLOCK = 256
AXES = ("seq", "head")
GROUP = 16
STREAMS = 4


def split_hi_lo(x):
    hi = lax.reduce_precision(x, exponent_bits=8, mantissa_bits=7)
    return hi.astype(jnp.bfloat16), (x - hi).astype(jnp.bfloat16)


def kernel_split(x):
    hi = x.astype(jnp.bfloat16)
    return hi, (x - hi.astype(jnp.float32)).astype(jnp.bfloat16)


def state_kernel(rates_ref, k_ref, v_ref, out_ref):
    g = pl.program_id(0)
    span = k_ref.shape[0]
    tail = (span - 1.0) - lax.broadcasted_iota(jnp.int32, (span, 1), 0).astype(jnp.float32)
    for hh in range(GROUP):
        rate = rates_ref[g * GROUP + hh]
        cols = slice(hh * HEAD_DIM, (hh + 1) * HEAD_DIM)
        kd = k_ref[:, cols].astype(jnp.float32) * jnp.exp(-rate * tail)
        hi, lo = kernel_split(kd)
        both = lax.dot_general(
            v_ref[:, cols],
            jnp.concatenate([hi, lo], axis=1),
            (((0,), (0,)), ((), ())),
            preferred_element_type=jnp.float32,
        )
        out_ref[hh] = both[:, :HEAD_DIM] + both[:, HEAD_DIM:]


def block_state(decay_rates, k, v):
    span = k.shape[0]
    groups = HEADS // GROUP
    width = GROUP * HEAD_DIM
    return pl.pallas_call(
        state_kernel,
        grid=(groups,),
        in_specs=[
            pl.BlockSpec(memory_space=pltpu.SMEM),
            pl.BlockSpec((span, width), lambda g: (0, g)),
            pl.BlockSpec((span, width), lambda g: (0, g)),
        ],
        out_specs=pl.BlockSpec((GROUP, HEAD_DIM, HEAD_DIM), lambda g: (g, 0, 0)),
        out_shape=jax.ShapeDtypeStruct((HEADS, HEAD_DIM, HEAD_DIM), jnp.float32),
        cost_estimate=pl.CostEstimate(
            flops=4 * span * HEADS * HEAD_DIM * HEAD_DIM,
            transcendentals=span * HEADS * HEAD_DIM,
            bytes_accessed=2 * 2 * span * HEADS * HEAD_DIM + 4 * HEADS * HEAD_DIM * HEAD_DIM,
        ),
    )(decay_rates, k, v)


def intra_kernel(rates_ref, q_ref, k_ref, v_ref, out_ref):
    g = pl.program_id(0)
    span = q_ref.shape[0]
    rows = lax.broadcasted_iota(jnp.int32, (span, span), 0).astype(jnp.float32)
    cols_i = lax.broadcasted_iota(jnp.int32, (span, span), 1).astype(jnp.float32)
    offsets = rows - cols_i
    causal = offsets >= 0.0
    gap = jnp.maximum(offsets, 0.0)
    for hh in range(GROUP):
        rate = rates_ref[g * GROUP + hh]
        cols = slice(hh * HEAD_DIM, (hh + 1) * HEAD_DIM)
        q = q_ref[:, cols]
        k = k_ref[:, cols]
        scores = lax.dot_general(
            q, k, (((1,), (1,)), ((), ())), preferred_element_type=jnp.float32
        )
        within = jnp.where(causal, jnp.exp(-rate * gap), 0.0)
        weights = (scores * within).astype(jnp.bfloat16)
        out_ref[:, cols] = jnp.dot(weights, v_ref[:, cols], preferred_element_type=jnp.float32)


def block_intra(decay_rates, q, k, v):
    span = q.shape[0]
    groups = HEADS // GROUP
    width = GROUP * HEAD_DIM
    return pl.pallas_call(
        intra_kernel,
        grid=(groups,),
        in_specs=[
            pl.BlockSpec(memory_space=pltpu.SMEM),
            pl.BlockSpec((span, width), lambda g: (0, g)),
            pl.BlockSpec((span, width), lambda g: (0, g)),
            pl.BlockSpec((span, width), lambda g: (0, g)),
        ],
        out_specs=pl.BlockSpec((span, width), lambda g: (0, g)),
        out_shape=jax.ShapeDtypeStruct((span, HEADS * HEAD_DIM), jnp.float32),
        cost_estimate=pl.CostEstimate(
            flops=HEADS * 4 * span * span * HEAD_DIM,
            transcendentals=HEADS * span * span,
            bytes_accessed=3 * 2 * span * HEADS * HEAD_DIM + 4 * span * HEADS * HEAD_DIM,
        ),
    )(decay_rates, q, k, v)


def output_kernel(rates_ref, intra_ref, q_ref, s_ref, gain_ref, out_ref):
    g = pl.program_id(0)
    span = q_ref.shape[0]
    lead = lax.broadcasted_iota(jnp.int32, (span, 1), 0).astype(jnp.float32) + 1.0
    for hh in range(GROUP):
        rate = rates_ref[g * GROUP + hh]
        cols = slice(hh * HEAD_DIM, (hh + 1) * HEAD_DIM)
        q = q_ref[:, cols]
        hi, lo = kernel_split(s_ref[g * GROUP + hh])
        nt = (((1,), (1,)), ((), ()))
        inter = lax.dot_general(q, hi, nt, preferred_element_type=jnp.float32) + lax.dot_general(
            q, lo, nt, preferred_element_type=jnp.float32
        )
        total = intra_ref[:, cols] + inter * jnp.exp(-rate * lead)
        mean_square = jnp.mean(total * total, axis=-1, keepdims=True)
        normed = total * lax.rsqrt(mean_square + 1e-06) * gain_ref[pl.ds(g * GROUP + hh, 1), :]
        out_ref[:, cols] = normed.astype(out_ref.dtype)


def block_output(decay_rates, intra, q, incoming, gains):
    span = q.shape[0]
    groups = HEADS // GROUP
    width = GROUP * HEAD_DIM
    return pl.pallas_call(
        output_kernel,
        grid=(groups,),
        in_specs=[
            pl.BlockSpec(memory_space=pltpu.SMEM),
            pl.BlockSpec((span, width), lambda g: (0, g)),
            pl.BlockSpec((span, width), lambda g: (0, g)),
            pl.BlockSpec(memory_space=pltpu.VMEM),
            pl.BlockSpec(memory_space=pltpu.VMEM),
        ],
        out_specs=pl.BlockSpec((span, width), lambda g: (0, g)),
        out_shape=jax.ShapeDtypeStruct((span, HEADS * HEAD_DIM), jnp.bfloat16),
        cost_estimate=pl.CostEstimate(
            flops=HEADS * 4 * span * HEAD_DIM * HEAD_DIM,
            transcendentals=HEADS * span,
            bytes_accessed=8 * span * HEADS * HEAD_DIM + 4 * HEADS * HEAD_DIM * HEAD_DIM,
        ),
    )(decay_rates, intra, q, pltpu.with_memory_space_constraint(incoming, pltpu.VMEM), gains)


def chain_kernel(carry_ref, g_ref, out_hbm, out_vmem, out_sems):
    blocks = g_ref.shape[0]
    size = blocks // STREAMS
    stores = [
        pltpu.make_async_copy(
            out_vmem.at[pl.ds(p * size, size)], out_hbm.at[pl.ds(p * size, size)], out_sems.at[p]
        )
        for p in range(STREAMS)
    ]
    carry = carry_ref[0]
    state = jnp.zeros(g_ref.shape[1:], jnp.float32)
    out_vmem[0] = state

    def step(b, state):
        state = carry * state + g_ref[b - 1]
        out_vmem[b] = state
        return state

    for p in range(STREAMS):
        first = 1 if p == 0 else p * size
        state = lax.fori_loop(first, (p + 1) * size, step, state, unroll=8)
        stores[p].start()
    for copy in stores:
        copy.wait()


def block_chain(carry, gathered):
    blocks, rows, width = gathered.shape
    return pl.pallas_call(
        chain_kernel,
        in_specs=[
            pl.BlockSpec(memory_space=pltpu.SMEM),
            pl.BlockSpec(memory_space=pltpu.VMEM),
        ],
        out_specs=pl.BlockSpec(memory_space=pl.ANY),
        out_shape=jax.ShapeDtypeStruct((blocks, rows, width), jnp.float32),
        scratch_shapes=[
            pltpu.VMEM((blocks, rows, width), jnp.float32),
            pltpu.SemaphoreType.DMA((STREAMS,)),
        ],
        cost_estimate=pl.CostEstimate(
            flops=2 * blocks * rows * width,
            transcendentals=0,
            bytes_accessed=8 * blocks * rows * width,
        ),
    )(carry, pltpu.with_memory_space_constraint(gathered, pltpu.VMEM))


def body(n, queries, key_rows, value_rows, decay_rates, norm_gain):
    span = queries.shape[0]
    me = lax.axis_index(AXES)

    local_state = block_state(decay_rates, key_rows, value_rows)

    rows = HEADS * HEAD_DIM // n
    chunks = local_state.reshape(n, rows, HEAD_DIM)
    gathered = lax.all_to_all(chunks, AXES, 0, 0, tiled=True)
    intra = block_intra(decay_rates, queries, key_rows, value_rows)
    head_of_chunk = me // (n // HEADS)
    rate = lax.dynamic_slice_in_dim(decay_rates, head_of_chunk, 1)
    before = block_chain(jnp.exp(-rate * float(span)), gathered)
    incoming = lax.all_to_all(before, AXES, 0, 0, tiled=True)
    incoming = incoming.reshape(HEADS, HEAD_DIM, HEAD_DIM)

    gains = norm_gain.reshape(HEADS, HEAD_DIM)
    return block_output(decay_rates, intra, queries, incoming, gains)


def solution(mesh):
    n = mesh.shape["seq"] * mesh.shape["head"]

    def run(queries, key_rows, value_rows, decay_rates, norm_gain):
        return body(n, queries, key_rows, value_rows, decay_rates, norm_gain)

    return jax.shard_map(
        run,
        mesh=mesh,
        in_specs=(
            P(AXES, None),
            P(AXES, None),
            P(AXES, None),
            P(),
            P(),
        ),
        out_specs=P(AXES, None),
        check_vma=False,
    )
```

```python
import jax
import jax.numpy as jnp
from jax import lax
from jax.experimental import pallas as pl
from jax.experimental.pallas import tpu as pltpu
from jax.sharding import PartitionSpec as P

HEADS = 32
HEAD_DIM = 128
BLOCK = 256
AXES = ("seq", "head")
GROUP = 16
STREAMS = 4


def split_hi_lo(x):
    hi = lax.reduce_precision(x, exponent_bits=8, mantissa_bits=7)
    return hi.astype(jnp.bfloat16), (x - hi).astype(jnp.bfloat16)


def kernel_split(x):
    hi = x.astype(jnp.bfloat16)
    return hi, (x - hi.astype(jnp.float32)).astype(jnp.bfloat16)


def state_kernel(rates_ref, k_ref, v_ref, out_ref):
    g = pl.program_id(0)
    span = k_ref.shape[0]
    tail = (span - 1.0) - lax.broadcasted_iota(jnp.int32, (span, 1), 0).astype(jnp.float32)
    for hh in range(GROUP):
        rate = rates_ref[g * GROUP + hh]
        cols = slice(hh * HEAD_DIM, (hh + 1) * HEAD_DIM)
        kd = k_ref[:, cols].astype(jnp.float32) * jnp.exp(-rate * tail)
        hi, lo = kernel_split(kd)
        v = v_ref[:, cols]
        dims = (((0,), (0,)), ((), ()))
        out_ref[hh] = lax.dot_general(
            hi, v, dims, preferred_element_type=jnp.float32
        ) + lax.dot_general(lo, v, dims, preferred_element_type=jnp.float32)


def block_state(decay_rates, k, v):
    span = k.shape[0]
    groups = HEADS // GROUP
    width = GROUP * HEAD_DIM
    return pl.pallas_call(
        state_kernel,
        grid=(groups,),
        in_specs=[
            pl.BlockSpec(memory_space=pltpu.SMEM),
            pl.BlockSpec((span, width), lambda g: (0, g)),
            pl.BlockSpec((span, width), lambda g: (0, g)),
        ],
        out_specs=pl.BlockSpec((GROUP, HEAD_DIM, HEAD_DIM), lambda g: (g, 0, 0)),
        out_shape=jax.ShapeDtypeStruct((HEADS, HEAD_DIM, HEAD_DIM), jnp.float32),
        cost_estimate=pl.CostEstimate(
            flops=4 * span * HEADS * HEAD_DIM * HEAD_DIM,
            transcendentals=span * HEADS * HEAD_DIM,
            bytes_accessed=2 * 2 * span * HEADS * HEAD_DIM + 4 * HEADS * HEAD_DIM * HEAD_DIM,
        ),
    )(decay_rates, k, v)


def intra_kernel(rates_ref, q_ref, k_ref, v_ref, out_ref):
    g = pl.program_id(0)
    span = q_ref.shape[0]
    rows = lax.broadcasted_iota(jnp.int32, (span, span), 0).astype(jnp.float32)
    cols_i = lax.broadcasted_iota(jnp.int32, (span, span), 1).astype(jnp.float32)
    offsets = rows - cols_i
    causal = offsets >= 0.0
    gap = jnp.maximum(offsets, 0.0)
    for hh in range(GROUP):
        rate = rates_ref[g * GROUP + hh]
        cols = slice(hh * HEAD_DIM, (hh + 1) * HEAD_DIM)
        q = q_ref[:, cols]
        k = k_ref[:, cols]
        scores = lax.dot_general(
            q, k, (((1,), (1,)), ((), ())), preferred_element_type=jnp.float32
        )
        within = jnp.where(causal, jnp.exp(-rate * gap), 0.0)
        weights = (scores * within).astype(jnp.bfloat16)
        out_ref[:, cols] = jnp.dot(weights, v_ref[:, cols], preferred_element_type=jnp.float32)


def block_intra(decay_rates, q, k, v):
    span = q.shape[0]
    groups = HEADS // GROUP
    width = GROUP * HEAD_DIM
    return pl.pallas_call(
        intra_kernel,
        grid=(groups,),
        in_specs=[
            pl.BlockSpec(memory_space=pltpu.SMEM),
            pl.BlockSpec((span, width), lambda g: (0, g)),
            pl.BlockSpec((span, width), lambda g: (0, g)),
            pl.BlockSpec((span, width), lambda g: (0, g)),
        ],
        out_specs=pl.BlockSpec((span, width), lambda g: (0, g)),
        out_shape=jax.ShapeDtypeStruct((span, HEADS * HEAD_DIM), jnp.float32),
        cost_estimate=pl.CostEstimate(
            flops=HEADS * 4 * span * span * HEAD_DIM,
            transcendentals=HEADS * span * span,
            bytes_accessed=3 * 2 * span * HEADS * HEAD_DIM + 4 * span * HEADS * HEAD_DIM,
        ),
    )(decay_rates, q, k, v)


def output_kernel(rates_ref, intra_ref, q_ref, s_ref, gain_ref, out_ref):
    g = pl.program_id(0)
    span = q_ref.shape[0]
    lead = lax.broadcasted_iota(jnp.int32, (span, 1), 0).astype(jnp.float32) + 1.0
    for hh in range(GROUP):
        rate = rates_ref[g * GROUP + hh]
        cols = slice(hh * HEAD_DIM, (hh + 1) * HEAD_DIM)
        q = q_ref[:, cols]
        hi, lo = kernel_split(s_ref[g * GROUP + hh])
        inter = jnp.dot(q, hi, preferred_element_type=jnp.float32) + jnp.dot(
            q, lo, preferred_element_type=jnp.float32
        )
        total = intra_ref[:, cols] + inter * jnp.exp(-rate * lead)
        mean_square = jnp.mean(total * total, axis=-1, keepdims=True)
        normed = total * lax.rsqrt(mean_square + 1e-06) * gain_ref[pl.ds(g * GROUP + hh, 1), :]
        out_ref[:, cols] = normed.astype(out_ref.dtype)


def block_output(decay_rates, intra, q, incoming, gains):
    span = q.shape[0]
    groups = HEADS // GROUP
    width = GROUP * HEAD_DIM
    return pl.pallas_call(
        output_kernel,
        grid=(groups,),
        in_specs=[
            pl.BlockSpec(memory_space=pltpu.SMEM),
            pl.BlockSpec((span, width), lambda g: (0, g)),
            pl.BlockSpec((span, width), lambda g: (0, g)),
            pl.BlockSpec(memory_space=pltpu.VMEM),
            pl.BlockSpec(memory_space=pltpu.VMEM),
        ],
        out_specs=pl.BlockSpec((span, width), lambda g: (0, g)),
        out_shape=jax.ShapeDtypeStruct((span, HEADS * HEAD_DIM), jnp.bfloat16),
        cost_estimate=pl.CostEstimate(
            flops=HEADS * 4 * span * HEAD_DIM * HEAD_DIM,
            transcendentals=HEADS * span,
            bytes_accessed=8 * span * HEADS * HEAD_DIM + 4 * HEADS * HEAD_DIM * HEAD_DIM,
        ),
    )(decay_rates, intra, q, pltpu.with_memory_space_constraint(incoming, pltpu.VMEM), gains)


def chain_kernel(carry_ref, g_ref, out_hbm, out_vmem, out_sems):
    blocks = g_ref.shape[0]
    size = blocks // STREAMS
    stores = [
        pltpu.make_async_copy(
            out_vmem.at[pl.ds(p * size, size)], out_hbm.at[pl.ds(p * size, size)], out_sems.at[p]
        )
        for p in range(STREAMS)
    ]
    carry = carry_ref[0]
    carry2 = carry * carry
    state = jnp.zeros(g_ref.shape[1:], jnp.float32)
    out_vmem[0] = state

    def pair(i, state):
        b = 2 * i
        a0 = g_ref[b]
        a1 = g_ref[b + 1]
        out_vmem[b + 1] = carry * state + a0
        state = carry2 * state + (carry * a0 + a1)
        out_vmem[b + 2] = state
        return state

    for p in range(STREAMS):
        first = p * size // 2
        last = (p + 1) * size // 2 - (1 if p == STREAMS - 1 else 0)
        state = lax.fori_loop(first, last, pair, state, unroll=4)
        if p == STREAMS - 1:
            out_vmem[blocks - 1] = carry * state + g_ref[blocks - 2]
        stores[p].start()
    for copy in stores:
        copy.wait()


def block_chain(carry, gathered):
    blocks, rows, width = gathered.shape
    return pl.pallas_call(
        chain_kernel,
        in_specs=[
            pl.BlockSpec(memory_space=pltpu.SMEM),
            pl.BlockSpec(memory_space=pltpu.VMEM),
        ],
        out_specs=pl.BlockSpec(memory_space=pl.ANY),
        out_shape=jax.ShapeDtypeStruct((blocks, rows, width), jnp.float32),
        scratch_shapes=[
            pltpu.VMEM((blocks, rows, width), jnp.float32),
            pltpu.SemaphoreType.DMA((STREAMS,)),
        ],
        cost_estimate=pl.CostEstimate(
            flops=2 * blocks * rows * width,
            transcendentals=0,
            bytes_accessed=8 * blocks * rows * width,
        ),
    )(carry, pltpu.with_memory_space_constraint(gathered, pltpu.VMEM))


def body(n, queries, key_rows, value_rows, decay_rates, norm_gain):
    span = queries.shape[0]
    me = lax.axis_index(AXES)

    local_state = block_state(decay_rates, key_rows, value_rows)

    rows = HEADS * HEAD_DIM // n
    chunks = local_state.reshape(n, rows, HEAD_DIM)
    gathered = lax.all_to_all(chunks, AXES, 0, 0, tiled=True)
    intra = block_intra(decay_rates, queries, key_rows, value_rows)
    head_of_chunk = me // (n // HEADS)
    rate = lax.dynamic_slice_in_dim(decay_rates, head_of_chunk, 1)
    before = block_chain(jnp.exp(-rate * float(span)), gathered)
    incoming = lax.all_to_all(before, AXES, 0, 0, tiled=True)
    incoming = incoming.reshape(HEADS, HEAD_DIM, HEAD_DIM)

    gains = norm_gain.reshape(HEADS, HEAD_DIM)
    return block_output(decay_rates, intra, queries, incoming, gains)


def solution(mesh):
    n = mesh.shape["seq"] * mesh.shape["head"]

    def run(queries, key_rows, value_rows, decay_rates, norm_gain):
        return body(n, queries, key_rows, value_rows, decay_rates, norm_gain)

    return jax.shard_map(
        run,
        mesh=mesh,
        in_specs=(
            P(AXES, None),
            P(AXES, None),
            P(AXES, None),
            P(),
            P(),
        ),
        out_specs=P(AXES, None),
        check_vma=False,
    )
```

```python
import jax
import jax.numpy as jnp
from jax import lax
from jax.experimental import pallas as pl
from jax.experimental.pallas import tpu as pltpu
from jax.sharding import PartitionSpec as P

HEADS = 32
HEAD_DIM = 128
BLOCK = 256
AXES = ("seq", "head")
GROUP = 16
ROW_STEPS = 2
STREAMS = 4


def split_hi_lo(x):
    hi = lax.reduce_precision(x, exponent_bits=8, mantissa_bits=7)
    return hi.astype(jnp.bfloat16), (x - hi).astype(jnp.bfloat16)


def kernel_split(x):
    hi = x.astype(jnp.bfloat16)
    return hi, (x - hi.astype(jnp.float32)).astype(jnp.bfloat16)


def state_kernel(rates_ref, k_ref, v_ref, out_ref):
    g = pl.program_id(0)
    span = k_ref.shape[0]
    tail = (span - 1.0) - lax.broadcasted_iota(jnp.int32, (span, 1), 0).astype(jnp.float32)
    for hh in range(GROUP):
        rate = rates_ref[g * GROUP + hh]
        cols = slice(hh * HEAD_DIM, (hh + 1) * HEAD_DIM)
        kd = k_ref[:, cols].astype(jnp.float32) * jnp.exp(-rate * tail)
        hi, lo = kernel_split(kd)
        v = v_ref[:, cols]
        dims = (((0,), (0,)), ((), ()))
        out_ref[hh] = lax.dot_general(
            hi, v, dims, preferred_element_type=jnp.float32
        ) + lax.dot_general(lo, v, dims, preferred_element_type=jnp.float32)


def block_state(decay_rates, k, v):
    span = k.shape[0]
    groups = HEADS // GROUP
    width = GROUP * HEAD_DIM
    return pl.pallas_call(
        state_kernel,
        grid=(groups,),
        in_specs=[
            pl.BlockSpec(memory_space=pltpu.SMEM),
            pl.BlockSpec((span, width), lambda g: (0, g)),
            pl.BlockSpec((span, width), lambda g: (0, g)),
        ],
        out_specs=pl.BlockSpec((GROUP, HEAD_DIM, HEAD_DIM), lambda g: (g, 0, 0)),
        out_shape=jax.ShapeDtypeStruct((HEADS, HEAD_DIM, HEAD_DIM), jnp.float32),
        cost_estimate=pl.CostEstimate(
            flops=4 * span * HEADS * HEAD_DIM * HEAD_DIM,
            transcendentals=span * HEADS * HEAD_DIM,
            bytes_accessed=2 * 2 * span * HEADS * HEAD_DIM + 4 * HEADS * HEAD_DIM * HEAD_DIM,
        ),
    )(decay_rates, k, v)


def intra_kernel(rates_ref, q_ref, k_ref, v_ref, out_ref):
    g = pl.program_id(0)
    span = q_ref.shape[0]
    rows = lax.broadcasted_iota(jnp.int32, (span, span), 0).astype(jnp.float32)
    cols_i = lax.broadcasted_iota(jnp.int32, (span, span), 1).astype(jnp.float32)
    offsets = rows - cols_i
    causal = offsets >= 0.0
    gap = jnp.maximum(offsets, 0.0)
    for hh in range(GROUP):
        rate = rates_ref[g * GROUP + hh]
        cols = slice(hh * HEAD_DIM, (hh + 1) * HEAD_DIM)
        q = q_ref[:, cols]
        k = k_ref[:, cols]
        scores = lax.dot_general(
            q, k, (((1,), (1,)), ((), ())), preferred_element_type=jnp.float32
        )
        within = jnp.where(causal, jnp.exp(-rate * gap), 0.0)
        weights = (scores * within).astype(jnp.bfloat16)
        out_ref[:, cols] = jnp.dot(weights, v_ref[:, cols], preferred_element_type=jnp.float32)


def block_intra(decay_rates, q, k, v):
    span = q.shape[0]
    groups = HEADS // GROUP
    width = GROUP * HEAD_DIM
    return pl.pallas_call(
        intra_kernel,
        grid=(groups,),
        in_specs=[
            pl.BlockSpec(memory_space=pltpu.SMEM),
            pl.BlockSpec((span, width), lambda g: (0, g)),
            pl.BlockSpec((span, width), lambda g: (0, g)),
            pl.BlockSpec((span, width), lambda g: (0, g)),
        ],
        out_specs=pl.BlockSpec((span, width), lambda g: (0, g)),
        out_shape=jax.ShapeDtypeStruct((span, HEADS * HEAD_DIM), jnp.float32),
        cost_estimate=pl.CostEstimate(
            flops=HEADS * 4 * span * span * HEAD_DIM,
            transcendentals=HEADS * span * span,
            bytes_accessed=3 * 2 * span * HEADS * HEAD_DIM + 4 * span * HEADS * HEAD_DIM,
        ),
    )(decay_rates, q, k, v)


def output_kernel(rates_ref, intra_ref, q_ref, s_ref, gain_ref, out_ref):
    g = pl.program_id(0)
    r = pl.program_id(1)
    rows = q_ref.shape[0]
    lead = lax.broadcasted_iota(jnp.int32, (rows, 1), 0).astype(jnp.float32) + (
        r * rows + 1
    ).astype(jnp.float32)
    for hh in range(GROUP):
        rate = rates_ref[g * GROUP + hh]
        cols = slice(hh * HEAD_DIM, (hh + 1) * HEAD_DIM)
        q = q_ref[:, cols]
        hi, lo = kernel_split(s_ref[g * GROUP + hh])
        inter = jnp.dot(q, hi, preferred_element_type=jnp.float32) + jnp.dot(
            q, lo, preferred_element_type=jnp.float32
        )
        total = intra_ref[:, cols] + inter * jnp.exp(-rate * lead)
        mean_square = jnp.mean(total * total, axis=-1, keepdims=True)
        normed = total * lax.rsqrt(mean_square + 1e-06) * gain_ref[pl.ds(g * GROUP + hh, 1), :]
        out_ref[:, cols] = normed.astype(out_ref.dtype)


def block_output(decay_rates, intra, q, incoming, gains):
    span = q.shape[0]
    groups = HEADS // GROUP
    width = GROUP * HEAD_DIM
    rows = span // ROW_STEPS
    tile = pl.BlockSpec((rows, width), lambda g, r: (r, g))
    return pl.pallas_call(
        output_kernel,
        grid=(groups, ROW_STEPS),
        in_specs=[
            pl.BlockSpec(memory_space=pltpu.SMEM),
            tile,
            tile,
            pl.BlockSpec(memory_space=pltpu.VMEM),
            pl.BlockSpec(memory_space=pltpu.VMEM),
        ],
        out_specs=tile,
        out_shape=jax.ShapeDtypeStruct((span, HEADS * HEAD_DIM), jnp.bfloat16),
        cost_estimate=pl.CostEstimate(
            flops=HEADS * 4 * span * HEAD_DIM * HEAD_DIM,
            transcendentals=HEADS * span,
            bytes_accessed=8 * span * HEADS * HEAD_DIM + 4 * HEADS * HEAD_DIM * HEAD_DIM,
        ),
    )(decay_rates, intra, q, pltpu.with_memory_space_constraint(incoming, pltpu.VMEM), gains)


def chain_kernel(carry_ref, g_ref, out_hbm, out_vmem, out_sems):
    blocks = g_ref.shape[0]
    size = blocks // STREAMS
    stores = [
        pltpu.make_async_copy(
            out_vmem.at[pl.ds(p * size, size)], out_hbm.at[pl.ds(p * size, size)], out_sems.at[p]
        )
        for p in range(STREAMS)
    ]
    carry = carry_ref[0]
    state = jnp.zeros(g_ref.shape[1:], jnp.float32)
    out_vmem[0] = state

    def step(b, state):
        state = carry * state + g_ref[b - 1]
        out_vmem[b] = state
        return state

    for p in range(STREAMS):
        first = 1 if p == 0 else p * size
        state = lax.fori_loop(first, (p + 1) * size, step, state, unroll=8)
        stores[p].start()
    for copy in stores:
        copy.wait()


def block_chain(carry, gathered):
    blocks, rows, width = gathered.shape
    return pl.pallas_call(
        chain_kernel,
        in_specs=[
            pl.BlockSpec(memory_space=pltpu.SMEM),
            pl.BlockSpec(memory_space=pltpu.VMEM),
        ],
        out_specs=pl.BlockSpec(memory_space=pl.ANY),
        out_shape=jax.ShapeDtypeStruct((blocks, rows, width), jnp.float32),
        scratch_shapes=[
            pltpu.VMEM((blocks, rows, width), jnp.float32),
            pltpu.SemaphoreType.DMA((STREAMS,)),
        ],
        cost_estimate=pl.CostEstimate(
            flops=2 * blocks * rows * width,
            transcendentals=0,
            bytes_accessed=8 * blocks * rows * width,
        ),
    )(carry, pltpu.with_memory_space_constraint(gathered, pltpu.VMEM))


def body(n, queries, key_rows, value_rows, decay_rates, norm_gain):
    span = queries.shape[0]
    me = lax.axis_index(AXES)

    local_state = block_state(decay_rates, key_rows, value_rows)

    rows = HEADS * HEAD_DIM // n
    chunks = local_state.reshape(n, rows, HEAD_DIM)
    gathered = lax.all_to_all(chunks, AXES, 0, 0, tiled=True)
    intra = block_intra(decay_rates, queries, key_rows, value_rows)
    head_of_chunk = me // (n // HEADS)
    rate = lax.dynamic_slice_in_dim(decay_rates, head_of_chunk, 1)
    before = block_chain(jnp.exp(-rate * float(span)), gathered)
    incoming = lax.all_to_all(before, AXES, 0, 0, tiled=True)
    incoming = incoming.reshape(HEADS, HEAD_DIM, HEAD_DIM)

    gains = norm_gain.reshape(HEADS, HEAD_DIM)
    return block_output(decay_rates, intra, queries, incoming, gains)


def solution(mesh):
    n = mesh.shape["seq"] * mesh.shape["head"]

    def run(queries, key_rows, value_rows, decay_rates, norm_gain):
        return body(n, queries, key_rows, value_rows, decay_rates, norm_gain)

    return jax.shard_map(
        run,
        mesh=mesh,
        in_specs=(
            P(AXES, None),
            P(AXES, None),
            P(AXES, None),
            P(),
            P(),
        ),
        out_specs=P(AXES, None),
        check_vma=False,
    )
```

```python
import jax
import jax.numpy as jnp
from jax import lax
from jax.experimental import pallas as pl
from jax.experimental.pallas import tpu as pltpu
from jax.sharding import PartitionSpec as P

HEADS = 32
HEAD_DIM = 128
BLOCK = 256
AXES = ("seq", "head")
GROUP = 16
OUT_PARTS = 2
STREAMS = 4


def split_hi_lo(x):
    hi = lax.reduce_precision(x, exponent_bits=8, mantissa_bits=7)
    return hi.astype(jnp.bfloat16), (x - hi).astype(jnp.bfloat16)


def kernel_split(x):
    hi = x.astype(jnp.bfloat16)
    return hi, (x - hi.astype(jnp.float32)).astype(jnp.bfloat16)


def state_kernel(rates_ref, k_ref, v_ref, out_ref):
    g = pl.program_id(0)
    span = k_ref.shape[0]
    tail = (span - 1.0) - lax.broadcasted_iota(jnp.int32, (span, 1), 0).astype(jnp.float32)
    for hh in range(GROUP):
        rate = rates_ref[g * GROUP + hh]
        cols = slice(hh * HEAD_DIM, (hh + 1) * HEAD_DIM)
        kd = k_ref[:, cols].astype(jnp.float32) * jnp.exp(-rate * tail)
        hi, lo = kernel_split(kd)
        v = v_ref[:, cols]
        dims = (((0,), (0,)), ((), ()))
        out_ref[hh] = lax.dot_general(
            hi, v, dims, preferred_element_type=jnp.float32
        ) + lax.dot_general(lo, v, dims, preferred_element_type=jnp.float32)


def block_state(decay_rates, k, v):
    span = k.shape[0]
    groups = HEADS // GROUP
    width = GROUP * HEAD_DIM
    return pl.pallas_call(
        state_kernel,
        grid=(groups,),
        in_specs=[
            pl.BlockSpec(memory_space=pltpu.SMEM),
            pl.BlockSpec((span, width), lambda g: (0, g)),
            pl.BlockSpec((span, width), lambda g: (0, g)),
        ],
        out_specs=pl.BlockSpec((GROUP, HEAD_DIM, HEAD_DIM), lambda g: (g, 0, 0)),
        out_shape=jax.ShapeDtypeStruct((HEADS, HEAD_DIM, HEAD_DIM), jnp.float32),
        cost_estimate=pl.CostEstimate(
            flops=4 * span * HEADS * HEAD_DIM * HEAD_DIM,
            transcendentals=span * HEADS * HEAD_DIM,
            bytes_accessed=2 * 2 * span * HEADS * HEAD_DIM + 4 * HEADS * HEAD_DIM * HEAD_DIM,
        ),
    )(decay_rates, k, v)


def intra_kernel(rates_ref, q_ref, k_ref, v_ref, out_ref):
    g = pl.program_id(0)
    span = q_ref.shape[0]
    rows = lax.broadcasted_iota(jnp.int32, (span, span), 0).astype(jnp.float32)
    cols_i = lax.broadcasted_iota(jnp.int32, (span, span), 1).astype(jnp.float32)
    offsets = rows - cols_i
    causal = offsets >= 0.0
    gap = jnp.maximum(offsets, 0.0)
    for hh in range(GROUP):
        rate = rates_ref[g * GROUP + hh]
        cols = slice(hh * HEAD_DIM, (hh + 1) * HEAD_DIM)
        q = q_ref[:, cols]
        k = k_ref[:, cols]
        scores = lax.dot_general(
            q, k, (((1,), (1,)), ((), ())), preferred_element_type=jnp.float32
        )
        within = jnp.where(causal, jnp.exp(-rate * gap), 0.0)
        weights = (scores * within).astype(jnp.bfloat16)
        out_ref[:, cols] = jnp.dot(weights, v_ref[:, cols], preferred_element_type=jnp.float32)


def block_intra(decay_rates, q, k, v):
    span = q.shape[0]
    groups = HEADS // GROUP
    width = GROUP * HEAD_DIM
    return pl.pallas_call(
        intra_kernel,
        grid=(groups,),
        in_specs=[
            pl.BlockSpec(memory_space=pltpu.SMEM),
            pl.BlockSpec((span, width), lambda g: (0, g)),
            pl.BlockSpec((span, width), lambda g: (0, g)),
            pl.BlockSpec((span, width), lambda g: (0, g)),
        ],
        out_specs=pl.BlockSpec((span, width), lambda g: (0, g)),
        out_shape=jax.ShapeDtypeStruct((span, HEADS * HEAD_DIM), jnp.float32),
        cost_estimate=pl.CostEstimate(
            flops=HEADS * 4 * span * span * HEAD_DIM,
            transcendentals=HEADS * span * span,
            bytes_accessed=3 * 2 * span * HEADS * HEAD_DIM + 4 * span * HEADS * HEAD_DIM,
        ),
    )(decay_rates, q, k, v)


def output_kernel(rates_ref, intra_ref, q_ref, s_ref, gain_ref, out_hbm, out_vmem, sems):
    g = pl.program_id(0)
    span = q_ref.shape[0]
    lead = lax.broadcasted_iota(jnp.int32, (span, 1), 0).astype(jnp.float32) + 1.0
    part = GROUP // OUT_PARTS
    width = part * HEAD_DIM
    copies = []
    for c in range(OUT_PARTS):
        for hh in range(c * part, (c + 1) * part):
            rate = rates_ref[g * GROUP + hh]
            cols = slice(hh * HEAD_DIM, (hh + 1) * HEAD_DIM)
            q = q_ref[:, cols]
            hi, lo = kernel_split(s_ref[g * GROUP + hh])
            inter = jnp.dot(q, hi, preferred_element_type=jnp.float32) + jnp.dot(
                q, lo, preferred_element_type=jnp.float32
            )
            total = intra_ref[:, cols] + inter * jnp.exp(-rate * lead)
            mean_square = jnp.mean(total * total, axis=-1, keepdims=True)
            normed = total * lax.rsqrt(mean_square + 1e-06) * gain_ref[pl.ds(g * GROUP + hh, 1), :]
            out_vmem[:, cols] = normed.astype(out_vmem.dtype)
        start = pl.multiple_of((g * GROUP + c * part) * HEAD_DIM, width)
        copy = pltpu.make_async_copy(
            out_vmem.at[:, pl.ds(c * width, width)], out_hbm.at[:, pl.ds(start, width)], sems.at[c]
        )
        copy.start()
        copies.append(copy)
    for copy in copies:
        copy.wait()


def block_output(decay_rates, intra, q, incoming, gains):
    span = q.shape[0]
    groups = HEADS // GROUP
    width = GROUP * HEAD_DIM
    return pl.pallas_call(
        output_kernel,
        grid=(groups,),
        in_specs=[
            pl.BlockSpec(memory_space=pltpu.SMEM),
            pl.BlockSpec((span, width), lambda g: (0, g)),
            pl.BlockSpec((span, width), lambda g: (0, g)),
            pl.BlockSpec(memory_space=pltpu.VMEM),
            pl.BlockSpec(memory_space=pltpu.VMEM),
        ],
        out_specs=pl.BlockSpec(memory_space=pl.ANY),
        out_shape=jax.ShapeDtypeStruct((span, HEADS * HEAD_DIM), jnp.bfloat16),
        scratch_shapes=[
            pltpu.VMEM((span, width), jnp.bfloat16),
            pltpu.SemaphoreType.DMA((OUT_PARTS,)),
        ],
        cost_estimate=pl.CostEstimate(
            flops=HEADS * 4 * span * HEAD_DIM * HEAD_DIM,
            transcendentals=HEADS * span,
            bytes_accessed=8 * span * HEADS * HEAD_DIM + 4 * HEADS * HEAD_DIM * HEAD_DIM,
        ),
    )(decay_rates, intra, q, pltpu.with_memory_space_constraint(incoming, pltpu.VMEM), gains)


def chain_kernel(carry_ref, g_ref, out_hbm, out_vmem, out_sems):
    blocks = g_ref.shape[0]
    size = blocks // STREAMS
    stores = [
        pltpu.make_async_copy(
            out_vmem.at[pl.ds(p * size, size)], out_hbm.at[pl.ds(p * size, size)], out_sems.at[p]
        )
        for p in range(STREAMS)
    ]
    carry = carry_ref[0]
    state = jnp.zeros(g_ref.shape[1:], jnp.float32)
    out_vmem[0] = state

    def step(b, state):
        state = carry * state + g_ref[b - 1]
        out_vmem[b] = state
        return state

    for p in range(STREAMS):
        first = 1 if p == 0 else p * size
        state = lax.fori_loop(first, (p + 1) * size, step, state, unroll=8)
        stores[p].start()
    for copy in stores:
        copy.wait()


def block_chain(carry, gathered):
    blocks, rows, width = gathered.shape
    return pl.pallas_call(
        chain_kernel,
        in_specs=[
            pl.BlockSpec(memory_space=pltpu.SMEM),
            pl.BlockSpec(memory_space=pltpu.VMEM),
        ],
        out_specs=pl.BlockSpec(memory_space=pl.ANY),
        out_shape=jax.ShapeDtypeStruct((blocks, rows, width), jnp.float32),
        scratch_shapes=[
            pltpu.VMEM((blocks, rows, width), jnp.float32),
            pltpu.SemaphoreType.DMA((STREAMS,)),
        ],
        cost_estimate=pl.CostEstimate(
            flops=2 * blocks * rows * width,
            transcendentals=0,
            bytes_accessed=8 * blocks * rows * width,
        ),
    )(carry, pltpu.with_memory_space_constraint(gathered, pltpu.VMEM))


def body(n, queries, key_rows, value_rows, decay_rates, norm_gain):
    span = queries.shape[0]
    me = lax.axis_index(AXES)

    local_state = block_state(decay_rates, key_rows, value_rows)

    rows = HEADS * HEAD_DIM // n
    chunks = local_state.reshape(n, rows, HEAD_DIM)
    gathered = lax.all_to_all(chunks, AXES, 0, 0, tiled=True)
    intra = block_intra(decay_rates, queries, key_rows, value_rows)
    head_of_chunk = me // (n // HEADS)
    rate = lax.dynamic_slice_in_dim(decay_rates, head_of_chunk, 1)
    before = block_chain(jnp.exp(-rate * float(span)), gathered)
    incoming = lax.all_to_all(before, AXES, 0, 0, tiled=True)
    incoming = incoming.reshape(HEADS, HEAD_DIM, HEAD_DIM)

    gains = norm_gain.reshape(HEADS, HEAD_DIM)
    return block_output(decay_rates, intra, queries, incoming, gains)


def solution(mesh):
    n = mesh.shape["seq"] * mesh.shape["head"]

    def run(queries, key_rows, value_rows, decay_rates, norm_gain):
        return body(n, queries, key_rows, value_rows, decay_rates, norm_gain)

    return jax.shard_map(
        run,
        mesh=mesh,
        in_specs=(
            P(AXES, None),
            P(AXES, None),
            P(AXES, None),
            P(),
            P(),
        ),
        out_specs=P(AXES, None),
        check_vma=False,
    )
```

```python
import jax
import jax.numpy as jnp
from jax import lax
from jax.experimental import pallas as pl
from jax.experimental.pallas import tpu as pltpu
from jax.sharding import PartitionSpec as P

HEADS = 32
HEAD_DIM = 128
BLOCK = 256
AXES = ("seq", "head")
GROUP = 16
STREAMS = 4


def split_hi_lo(x):
    hi = lax.reduce_precision(x, exponent_bits=8, mantissa_bits=7)
    return hi.astype(jnp.bfloat16), (x - hi).astype(jnp.bfloat16)


def kernel_split(x):
    hi = x.astype(jnp.bfloat16)
    return hi, (x - hi.astype(jnp.float32)).astype(jnp.bfloat16)


def state_kernel(rates_ref, k_ref, v_ref, out_ref):
    g = pl.program_id(0)
    span = k_ref.shape[0]
    tail = (span - 1.0) - lax.broadcasted_iota(jnp.int32, (span, 1), 0).astype(jnp.float32)
    for hh in range(GROUP):
        rate = rates_ref[g * GROUP + hh]
        cols = slice(hh * HEAD_DIM, (hh + 1) * HEAD_DIM)
        kd = k_ref[:, cols].astype(jnp.float32) * jnp.exp(-rate * tail)
        hi, lo = kernel_split(kd)
        v = v_ref[:, cols]
        dims = (((0,), (0,)), ((), ()))
        out_ref[hh] = lax.dot_general(
            hi, v, dims, preferred_element_type=jnp.float32
        ) + lax.dot_general(lo, v, dims, preferred_element_type=jnp.float32)


def block_state(decay_rates, k, v):
    span = k.shape[0]
    groups = HEADS // GROUP
    width = GROUP * HEAD_DIM
    return pl.pallas_call(
        state_kernel,
        grid=(groups,),
        in_specs=[
            pl.BlockSpec(memory_space=pltpu.SMEM),
            pl.BlockSpec((span, width), lambda g: (0, g)),
            pl.BlockSpec((span, width), lambda g: (0, g)),
        ],
        out_specs=pl.BlockSpec((GROUP, HEAD_DIM, HEAD_DIM), lambda g: (g, 0, 0)),
        out_shape=jax.ShapeDtypeStruct((HEADS, HEAD_DIM, HEAD_DIM), jnp.float32),
        cost_estimate=pl.CostEstimate(
            flops=4 * span * HEADS * HEAD_DIM * HEAD_DIM,
            transcendentals=span * HEADS * HEAD_DIM,
            bytes_accessed=2 * 2 * span * HEADS * HEAD_DIM + 4 * HEADS * HEAD_DIM * HEAD_DIM,
        ),
    )(decay_rates, k, v)


def intra_kernel(rates_ref, q_ref, k_ref, v_ref, out_ref):
    g = pl.program_id(0)
    span = q_ref.shape[0]
    rows = lax.broadcasted_iota(jnp.int32, (span, span), 0).astype(jnp.float32)
    cols_i = lax.broadcasted_iota(jnp.int32, (span, span), 1).astype(jnp.float32)
    offsets = rows - cols_i
    causal = offsets >= 0.0
    gap = jnp.maximum(offsets, 0.0)
    for hh in range(GROUP):
        rate = rates_ref[g * GROUP + hh]
        cols = slice(hh * HEAD_DIM, (hh + 1) * HEAD_DIM)
        q = q_ref[:, cols]
        k = k_ref[:, cols]
        scores = lax.dot_general(
            q, k, (((1,), (1,)), ((), ())), preferred_element_type=jnp.float32
        )
        within = jnp.where(causal, jnp.exp(-rate * gap), 0.0)
        weights = (scores * within).astype(jnp.bfloat16)
        out_ref[:, cols] = jnp.dot(weights, v_ref[:, cols], preferred_element_type=jnp.float32)


def block_intra(decay_rates, q, k, v):
    span = q.shape[0]
    groups = HEADS // GROUP
    width = GROUP * HEAD_DIM
    return pl.pallas_call(
        intra_kernel,
        grid=(groups,),
        in_specs=[
            pl.BlockSpec(memory_space=pltpu.SMEM),
            pl.BlockSpec((span, width), lambda g: (0, g)),
            pl.BlockSpec((span, width), lambda g: (0, g)),
            pl.BlockSpec((span, width), lambda g: (0, g)),
        ],
        out_specs=pl.BlockSpec((span, width), lambda g: (0, g)),
        out_shape=jax.ShapeDtypeStruct((span, HEADS * HEAD_DIM), jnp.float32),
        cost_estimate=pl.CostEstimate(
            flops=HEADS * 4 * span * span * HEAD_DIM,
            transcendentals=HEADS * span * span,
            bytes_accessed=3 * 2 * span * HEADS * HEAD_DIM + 4 * span * HEADS * HEAD_DIM,
        ),
    )(decay_rates, q, k, v)


def output_kernel(rates_ref, intra_ref, q_ref, s_ref, gain_ref, out_ref):
    g = pl.program_id(0)
    span = q_ref.shape[0]
    lead = lax.broadcasted_iota(jnp.int32, (span, 1), 0).astype(jnp.float32) + 1.0
    for hh in range(GROUP):
        rate = rates_ref[g * GROUP + hh]
        cols = slice(hh * HEAD_DIM, (hh + 1) * HEAD_DIM)
        q = q_ref[:, cols]
        hi, lo = kernel_split(s_ref[g * GROUP + hh])
        inter = jnp.dot(q, hi, preferred_element_type=jnp.float32) + jnp.dot(
            q, lo, preferred_element_type=jnp.float32
        )
        total = intra_ref[:, cols] + inter * jnp.exp(-rate * lead)
        mean_square = jnp.mean(total * total, axis=-1, keepdims=True)
        normed = total * lax.rsqrt(mean_square + 1e-06) * gain_ref[pl.ds(g * GROUP + hh, 1), :]
        out_ref[:, cols] = normed.astype(out_ref.dtype)


def block_output(decay_rates, intra, q, incoming, gains):
    span = q.shape[0]
    groups = HEADS // GROUP
    width = GROUP * HEAD_DIM
    return pl.pallas_call(
        output_kernel,
        grid=(groups,),
        in_specs=[
            pl.BlockSpec(memory_space=pltpu.SMEM),
            pl.BlockSpec((span, width), lambda g: (0, g)),
            pl.BlockSpec((span, width), lambda g: (0, g)),
            pl.BlockSpec(memory_space=pltpu.VMEM),
            pl.BlockSpec(memory_space=pltpu.VMEM),
        ],
        out_specs=pl.BlockSpec((span, width), lambda g: (0, g)),
        out_shape=jax.ShapeDtypeStruct((span, HEADS * HEAD_DIM), jnp.bfloat16),
        cost_estimate=pl.CostEstimate(
            flops=HEADS * 4 * span * HEAD_DIM * HEAD_DIM,
            transcendentals=HEADS * span,
            bytes_accessed=8 * span * HEADS * HEAD_DIM + 4 * HEADS * HEAD_DIM * HEAD_DIM,
        ),
    )(decay_rates, intra, q, pltpu.with_memory_space_constraint(incoming, pltpu.VMEM), gains)


def chain_kernel(carry_ref, g_ref, after_ref, out_hbm, out_vmem, out_sems):
    blocks = g_ref.shape[0]
    size = blocks // STREAMS
    stores = [
        pltpu.make_async_copy(
            out_vmem.at[pl.ds(p * size, size)], out_hbm.at[pl.ds(p * size, size)], out_sems.at[p]
        )
        for p in range(STREAMS)
    ]
    carry = carry_ref[0]
    state = jnp.zeros(g_ref.shape[1:], jnp.float32)
    out_vmem[0] = state

    def step(b, state):
        state = carry * state + g_ref[b - 1]
        out_vmem[b] = state
        return state

    for p in range(STREAMS):
        first = 1 if p == 0 else p * size
        state = lax.fori_loop(first, (p + 1) * size, step, state, unroll=8)
        stores[p].start()
    for copy in stores:
        copy.wait()


def block_chain(carry, gathered, after):
    blocks, rows, width = gathered.shape
    return pl.pallas_call(
        chain_kernel,
        in_specs=[
            pl.BlockSpec(memory_space=pltpu.SMEM),
            pl.BlockSpec(memory_space=pltpu.VMEM),
            pl.BlockSpec(memory_space=pl.ANY),
        ],
        out_specs=pl.BlockSpec(memory_space=pl.ANY),
        out_shape=jax.ShapeDtypeStruct((blocks, rows, width), jnp.float32),
        scratch_shapes=[
            pltpu.VMEM((blocks, rows, width), jnp.float32),
            pltpu.SemaphoreType.DMA((STREAMS,)),
        ],
        cost_estimate=pl.CostEstimate(
            flops=2 * blocks * rows * width,
            transcendentals=0,
            bytes_accessed=8 * blocks * rows * width,
        ),
    )(carry, pltpu.with_memory_space_constraint(gathered, pltpu.VMEM), after)


def body(n, queries, key_rows, value_rows, decay_rates, norm_gain):
    span = queries.shape[0]
    me = lax.axis_index(AXES)

    local_state = block_state(decay_rates, key_rows, value_rows)

    rows = HEADS * HEAD_DIM // n
    chunks = local_state.reshape(n, rows, HEAD_DIM)
    gathered = lax.all_to_all(chunks, AXES, 0, 0, tiled=True)
    intra = block_intra(decay_rates, queries, key_rows, value_rows)
    head_of_chunk = me // (n // HEADS)
    rate = lax.dynamic_slice_in_dim(decay_rates, head_of_chunk, 1)
    before = block_chain(jnp.exp(-rate * float(span)), gathered, intra)
    incoming = lax.all_to_all(before, AXES, 0, 0, tiled=True)
    incoming = incoming.reshape(HEADS, HEAD_DIM, HEAD_DIM)

    gains = norm_gain.reshape(HEADS, HEAD_DIM)
    return block_output(decay_rates, intra, queries, incoming, gains)


def solution(mesh):
    n = mesh.shape["seq"] * mesh.shape["head"]

    def run(queries, key_rows, value_rows, decay_rates, norm_gain):
        return body(n, queries, key_rows, value_rows, decay_rates, norm_gain)

    return jax.shard_map(
        run,
        mesh=mesh,
        in_specs=(
            P(AXES, None),
            P(AXES, None),
            P(AXES, None),
            P(),
            P(),
        ),
        out_specs=P(AXES, None),
        check_vma=False,
    )
```

```python
import jax
import jax.numpy as jnp
from jax import lax
from jax.experimental import pallas as pl
from jax.experimental.pallas import tpu as pltpu
from jax.sharding import PartitionSpec as P

HEADS = 32
HEAD_DIM = 128
BLOCK = 256
AXES = ("seq", "head")
GROUP = 16
OUT_GROUP = GROUP // 2
STREAMS = 4


def split_hi_lo(x):
    hi = lax.reduce_precision(x, exponent_bits=8, mantissa_bits=7)
    return hi.astype(jnp.bfloat16), (x - hi).astype(jnp.bfloat16)


def kernel_split(x):
    hi = x.astype(jnp.bfloat16)
    return hi, (x - hi.astype(jnp.float32)).astype(jnp.bfloat16)


def state_kernel(rates_ref, k_ref, v_ref, out_ref):
    g = pl.program_id(0)
    span = k_ref.shape[0]
    half = g % 2
    tail = (span - 1.0) - lax.broadcasted_iota(jnp.int32, (span, 1), 0).astype(jnp.float32)
    dims = (((0,), (0,)), ((), ()))
    for hh in range(OUT_GROUP):
        rate = rates_ref[g * OUT_GROUP + hh]
        cols = pl.ds(pl.multiple_of((half * OUT_GROUP + hh) * HEAD_DIM, HEAD_DIM), HEAD_DIM)
        kd = k_ref[:, cols].astype(jnp.float32) * jnp.exp(-rate * tail)
        hi, lo = kernel_split(kd)
        v = v_ref[:, cols]
        out_ref[hh] = lax.dot_general(
            hi, v, dims, preferred_element_type=jnp.float32
        ) + lax.dot_general(lo, v, dims, preferred_element_type=jnp.float32)


def block_state(decay_rates, k, v):
    span = k.shape[0]
    width = GROUP * HEAD_DIM
    return pl.pallas_call(
        state_kernel,
        grid=(HEADS // OUT_GROUP,),
        in_specs=[
            pl.BlockSpec(memory_space=pltpu.SMEM),
            pl.BlockSpec((span, width), lambda g: (0, g // 2)),
            pl.BlockSpec((span, width), lambda g: (0, g // 2)),
        ],
        out_specs=pl.BlockSpec((OUT_GROUP, HEAD_DIM, HEAD_DIM), lambda g: (g, 0, 0)),
        out_shape=jax.ShapeDtypeStruct((HEADS, HEAD_DIM, HEAD_DIM), jnp.float32),
        cost_estimate=pl.CostEstimate(
            flops=4 * span * HEADS * HEAD_DIM * HEAD_DIM,
            transcendentals=span * HEADS * HEAD_DIM,
            bytes_accessed=2 * 2 * span * HEADS * HEAD_DIM + 4 * HEADS * HEAD_DIM * HEAD_DIM,
        ),
    )(decay_rates, k, v)


def intra_kernel(rates_ref, q_ref, k_ref, v_ref, out_ref):
    g = pl.program_id(0)
    span = q_ref.shape[0]
    rows = lax.broadcasted_iota(jnp.int32, (span, span), 0).astype(jnp.float32)
    cols_i = lax.broadcasted_iota(jnp.int32, (span, span), 1).astype(jnp.float32)
    offsets = rows - cols_i
    causal = offsets >= 0.0
    gap = jnp.maximum(offsets, 0.0)
    for hh in range(GROUP):
        rate = rates_ref[g * GROUP + hh]
        cols = slice(hh * HEAD_DIM, (hh + 1) * HEAD_DIM)
        q = q_ref[:, cols]
        k = k_ref[:, cols]
        scores = lax.dot_general(
            q, k, (((1,), (1,)), ((), ())), preferred_element_type=jnp.float32
        )
        within = jnp.where(causal, jnp.exp(-rate * gap), 0.0)
        weights = (scores * within).astype(jnp.bfloat16)
        out_ref[:, cols] = jnp.dot(weights, v_ref[:, cols], preferred_element_type=jnp.float32)


def block_intra(decay_rates, q, k, v):
    span = q.shape[0]
    groups = HEADS // GROUP
    width = GROUP * HEAD_DIM
    return pl.pallas_call(
        intra_kernel,
        grid=(groups,),
        in_specs=[
            pl.BlockSpec(memory_space=pltpu.SMEM),
            pl.BlockSpec((span, width), lambda g: (0, g)),
            pl.BlockSpec((span, width), lambda g: (0, g)),
            pl.BlockSpec((span, width), lambda g: (0, g)),
        ],
        out_specs=pl.BlockSpec((span, width), lambda g: (0, g)),
        out_shape=jax.ShapeDtypeStruct((span, HEADS * HEAD_DIM), jnp.float32),
        cost_estimate=pl.CostEstimate(
            flops=HEADS * 4 * span * span * HEAD_DIM,
            transcendentals=HEADS * span * span,
            bytes_accessed=3 * 2 * span * HEADS * HEAD_DIM + 4 * span * HEADS * HEAD_DIM,
        ),
    )(decay_rates, q, k, v)


def output_kernel(rates_ref, intra_ref, q_ref, s_ref, gain_ref, out_ref):
    g = pl.program_id(0)
    span = q_ref.shape[0]
    lead = lax.broadcasted_iota(jnp.int32, (span, 1), 0).astype(jnp.float32) + 1.0
    for hh in range(GROUP):
        rate = rates_ref[g * GROUP + hh]
        cols = slice(hh * HEAD_DIM, (hh + 1) * HEAD_DIM)
        q = q_ref[:, cols]
        hi, lo = kernel_split(s_ref[g * GROUP + hh])
        inter = jnp.dot(q, hi, preferred_element_type=jnp.float32) + jnp.dot(
            q, lo, preferred_element_type=jnp.float32
        )
        total = intra_ref[:, cols] + inter * jnp.exp(-rate * lead)
        mean_square = jnp.mean(total * total, axis=-1, keepdims=True)
        normed = total * lax.rsqrt(mean_square + 1e-06) * gain_ref[pl.ds(g * GROUP + hh, 1), :]
        out_ref[:, cols] = normed.astype(out_ref.dtype)


def block_output(decay_rates, intra, q, incoming, gains):
    span = q.shape[0]
    groups = HEADS // GROUP
    width = GROUP * HEAD_DIM
    return pl.pallas_call(
        output_kernel,
        grid=(groups,),
        in_specs=[
            pl.BlockSpec(memory_space=pltpu.SMEM),
            pl.BlockSpec((span, width), lambda g: (0, g)),
            pl.BlockSpec((span, width), lambda g: (0, g)),
            pl.BlockSpec(memory_space=pltpu.VMEM),
            pl.BlockSpec(memory_space=pltpu.VMEM),
        ],
        out_specs=pl.BlockSpec((span, width), lambda g: (0, g)),
        out_shape=jax.ShapeDtypeStruct((span, HEADS * HEAD_DIM), jnp.bfloat16),
        cost_estimate=pl.CostEstimate(
            flops=HEADS * 4 * span * HEAD_DIM * HEAD_DIM,
            transcendentals=HEADS * span,
            bytes_accessed=8 * span * HEADS * HEAD_DIM + 4 * HEADS * HEAD_DIM * HEAD_DIM,
        ),
    )(decay_rates, intra, q, pltpu.with_memory_space_constraint(incoming, pltpu.VMEM), gains)


def chain_kernel(carry_ref, g_ref, out_hbm, out_vmem, out_sems):
    blocks = g_ref.shape[0]
    size = blocks // STREAMS
    stores = [
        pltpu.make_async_copy(
            out_vmem.at[pl.ds(p * size, size)], out_hbm.at[pl.ds(p * size, size)], out_sems.at[p]
        )
        for p in range(STREAMS)
    ]
    carry = carry_ref[0]
    state = jnp.zeros(g_ref.shape[1:], jnp.float32)
    out_vmem[0] = state

    def step(b, state):
        state = carry * state + g_ref[b - 1]
        out_vmem[b] = state
        return state

    for p in range(STREAMS):
        first = 1 if p == 0 else p * size
        state = lax.fori_loop(first, (p + 1) * size, step, state, unroll=8)
        stores[p].start()
    for copy in stores:
        copy.wait()


def block_chain(carry, gathered):
    blocks, rows, width = gathered.shape
    return pl.pallas_call(
        chain_kernel,
        in_specs=[
            pl.BlockSpec(memory_space=pltpu.SMEM),
            pl.BlockSpec(memory_space=pltpu.VMEM),
        ],
        out_specs=pl.BlockSpec(memory_space=pl.ANY),
        out_shape=jax.ShapeDtypeStruct((blocks, rows, width), jnp.float32),
        scratch_shapes=[
            pltpu.VMEM((blocks, rows, width), jnp.float32),
            pltpu.SemaphoreType.DMA((STREAMS,)),
        ],
        cost_estimate=pl.CostEstimate(
            flops=2 * blocks * rows * width,
            transcendentals=0,
            bytes_accessed=8 * blocks * rows * width,
        ),
    )(carry, pltpu.with_memory_space_constraint(gathered, pltpu.VMEM))


def body(n, queries, key_rows, value_rows, decay_rates, norm_gain):
    span = queries.shape[0]
    me = lax.axis_index(AXES)

    local_state = block_state(decay_rates, key_rows, value_rows)

    rows = HEADS * HEAD_DIM // n
    chunks = local_state.reshape(n, rows, HEAD_DIM)
    gathered = lax.all_to_all(chunks, AXES, 0, 0, tiled=True)
    intra = block_intra(decay_rates, queries, key_rows, value_rows)
    head_of_chunk = me // (n // HEADS)
    rate = lax.dynamic_slice_in_dim(decay_rates, head_of_chunk, 1)
    before = block_chain(jnp.exp(-rate * float(span)), gathered)
    incoming = lax.all_to_all(before, AXES, 0, 0, tiled=True)
    incoming = incoming.reshape(HEADS, HEAD_DIM, HEAD_DIM)

    gains = norm_gain.reshape(HEADS, HEAD_DIM)
    return block_output(decay_rates, intra, queries, incoming, gains)


def solution(mesh):
    n = mesh.shape["seq"] * mesh.shape["head"]

    def run(queries, key_rows, value_rows, decay_rates, norm_gain):
        return body(n, queries, key_rows, value_rows, decay_rates, norm_gain)

    return jax.shard_map(
        run,
        mesh=mesh,
        in_specs=(
            P(AXES, None),
            P(AXES, None),
            P(AXES, None),
            P(),
            P(),
        ),
        out_specs=P(AXES, None),
        check_vma=False,
    )
```
